512 devices in a mesh: tm: 64 (over z, y), area: 8 (over x, core).
Axes of the slice: x: 4, y: 4, z: 16, core: 2. Of those that a mesh axis runs over, the one named last changes fastest.
Arguments:
- demand: float32 [256, 71680], P('tm', 'area'), may hold values from -6 to 6
- unit_cost: float32 [256, 65536], P('tm', 'area'), may hold values from -18 to 18
- ptdf_tiles: bfloat16 [192, 128, 256], P('area'), may hold values from -0.25 to 0.25
- tile_area: int32 [192, 1], replicated, may hold values from 0 to 7; in each aligned block of 24 rows (0 to 23, 24 to 47, ...) at most 6 rows name the same one
- tile_block: int32 [192], replicated, may hold values from 0 to 34
- tile_row: int32 [192], replicated, may hold values from 0 to 11
- unit_bus: int32 [65536], P('area'), may hold values from 0 to 8959
- unit_class: int32 [65536], P('area'), may hold values from 0 to 2
- power_cap: float32 [65536], P('area'), may hold values from 0.1 to 2
- line_limit: float32 [12288], P('area'), may hold values from 0.2 to 2
- smoother: float32 [3, 256], replicated, as said below
Outputs:
- power: float32 [256, 65536], P('tm', 'area')
- line_duals: float32 [256, 12288], P('tm', 'area')
- primal_rms: float32 [2], replicated
The draws below stay inside these ranges and needn't reach their ends.
Inputs may be any that keep to these rules, and one draw needn't show every extreme that they name: `tile_area`: among the 24 tiles of one holder, at most 6 have their column block in one area, and some holder reaches 6. `smoother`: row k is the first column of the inverse of (c1 I + L)(c2 I + L) / (c1 c2) of order 256, with L = 2 I - S - S^T the cyclic second difference and class constants 1e-5 <= c1 < c2 <= 1.
All inputs are finite; a program needn't handle non-finite values.
Results may differ from the reference program's by a relative error of at most 0.0028.
Values may be sent and summed in bfloat16 or wider, within the bound.
No kernel may reach another device: no remote copies, remote signals or barrier semaphores. Data moves between devices by JAX's collectives and lax.ppermute only.
A program may use at most 64 MiB of HBM per device.

```python
import math
import jax
import jax.numpy as jnp
import numpy as np

HORIZON = 256
UNIT_AREA = 8192
COL_BLOCKS = 35
PANEL_WIDTH = 256
BUS_AREA = 8960
ROW_BLOCKS = 12
LINE_BLOCK = 128
TILE_SLOTS = 24
CAPACITY = 6
CLASSES = 3
ITERATIONS = 2
UNITS = 65536
BUSES = 71680
LINES = 12288
TILES = 192
N_AREA = 8


def green_column(const, places):
    theta = jnp.log1p(const / 2.0 + jnp.sqrt(const + const * const / 4.0))
    upper = jnp.exp(-theta * places) + jnp.exp(-theta * (HORIZON - places))
    return upper / (2.0 * jnp.sinh(theta) * (1.0 - jnp.exp(-theta * HORIZON)))


def draw_smoother(key, part):
    base_key = jax.random.fold_in(key, 11)
    order_key, place_key, ratio_key = jax.random.split(base_key, 3)
    spread = jax.random.uniform(place_key, (CLASSES, 1), jnp.float32)
    bands = jax.random.permutation(order_key, CLASSES).astype(jnp.float32)[:, None]
    band_width = (math.log(0.1) - math.log(1e-05)) / CLASSES
    log_lower = math.log(1e-05) + (bands + spread) * band_width
    lower = jnp.exp(log_lower)
    higher = lower * jax.random.uniform(ratio_key, (CLASSES, 1), jnp.float32, 3.0, 10.0)
    places = jnp.arange(HORIZON, dtype=jnp.float32)[None, :]
    values = lower * higher * (green_column(lower, places) - green_column(higher, places)) / (higher - lower)
    return values.astype(jnp.float32)


def with_ends(drawn, own_key, least, high):
    spot = [jax.random.randint(jax.random.fold_in(own_key, axis), (), 0, length) for axis, length in enumerate(drawn.shape)]
    longest = drawn.shape.index(max(drawn.shape))
    beside = spot[:longest] + [(spot[longest] + 1) % drawn.shape[longest]] + spot[longest + 1:]
    return drawn.at[tuple(spot)].set(least).at[tuple(beside)].set(high)


def steps_of(stream_key, shape, pieces, low, top_value):
    def one(axis_at, shards_of):
        draws = jax.random.uniform(jax.random.fold_in(jax.random.fold_in(stream_key, 6), axis_at), (shards_of,), jnp.float32, low / len(pieces), top_value / len(pieces))
        return jnp.repeat(jnp.exp(draws), shape[axis_at] // shards_of).reshape((-1,) + (1,) * (len(shape) - axis_at - 1))

    loudness = one(*pieces[0])
    for cut in pieces[1:]:
        loudness = loudness * one(*cut)
    return loudness


def routed_block(own_key, own, number, rows, number_of, top, limit, skew):
    order = jax.random.permutation(own_key, number_of)
    heavy_load, ordinary = shares(number_of, rows * top, limit, skew, True), shares(number_of, rows * top, limit, skew, False)
    places = jnp.arange(number_of)

    def named(sizes, rotation):
        used = int((sizes > 0).sum())
        fixed = max(1, used // 4)
        shifted = fixed + (places - fixed + rotation * (used - fixed)) % max(1, number_of - fixed)
        return jnp.zeros((number_of,), jnp.int32).at[order[jnp.where(places < fixed, places, shifted)]].set(jnp.asarray(sizes, jnp.int32))

    sizes = jnp.where(number % 4 == 0, named(heavy_load, number // 4), named(ordinary, number - number // 4 - 1))
    mixed = jax.random.permutation(jax.random.fold_in(own, 3), number_of)
    source_of, taker = mixed[0:number_of // 2 * 2:2], mixed[1:number_of // 2 * 2:2]
    slack = jnp.minimum(sizes[source_of] - 1, limit - sizes[taker]) // 2
    slack = jnp.where((source_of == order[0]) | (taker == order[0]) | (sizes[taker] == 0), 0, jnp.maximum(slack, 0))
    shifted = jax.random.randint(jax.random.fold_in(own, 4), (number_of // 2,), 0, 1 << 20) % (slack + 1)
    sizes = sizes.at[source_of].add(-shifted).at[taker].add(shifted)
    labels = jnp.searchsorted(jnp.cumsum(sizes), jnp.arange(rows * top), side="right").astype(jnp.int32)
    listing = labels.reshape(top, rows).T
    listing = listing[jax.random.permutation(jax.random.fold_in(own, 1), rows)]
    rotation = jax.random.randint(jax.random.fold_in(own, 2), (rows, 1), 0, top)
    return jnp.take_along_axis(listing, (jnp.arange(top)[None, :] + rotation) % top, axis=1)


def shares(count, total, most, lean, full):
    weights = [(1 << 20) // math.isqrt(standing ** lean) + 1 for standing in range(1, count + 1)]
    largest = most if full else min(most, max(-(-total // count), total * weights[0] // sum(weights)))
    least = 1 if total - largest >= count - 1 else 0
    given, spare = [largest] + [least] * (count - 1), total - largest - least * (count - 1)
    while spare > 0:
        free = [i for i in range(1, count) if given[i] < largest] or [i for i in range(1, count) if given[i] < most]
        whole, remaining = sum([weights[i] for i in free]), spare
        for i in free:
            extra = min(most - given[i], max(1, remaining * weights[i] // whole), spare)
            given[i] = given[i] + extra
            spare = spare - extra
    return np.array(given)


def scatter_about(stream_key, shape, deviation, limit, shards=(), held_as=jnp.bfloat16):
    factor_of = steps_of(stream_key, shape, shards, -0.22, 0.18) if shards else 1.0
    entries = jax.random.normal(stream_key, shape, jnp.float32) * deviation * factor_of
    return jnp.minimum(jnp.maximum(entries, -limit), limit).astype(held_as)


def setup_inputs(seed: int = 0) -> dict:
    seeds = jax.random.split(jax.random.key(seed), 12)
    demand = scatter_about(seeds[0], (HORIZON, BUSES), 1.0, 6.0, ((0, 64), (1, 8)), jnp.float32)
    unit_cost = scatter_about(seeds[1], (HORIZON, UNITS), 3.0, 18.0, ((0, 64), (1, 8)), jnp.float32)
    ptdf_tiles = scatter_about(seeds[2], (TILES, LINE_BLOCK, PANEL_WIDTH), (2 * PANEL_WIDTH) ** -0.5, 0.25, ((0, 8),))
    tile_area_keys = jax.random.split(jax.random.fold_in(seeds[3], 1), TILES // TILE_SLOTS)
    tile_area_turns = jax.random.permutation(jax.random.fold_in(seeds[3], 3), TILES // TILE_SLOTS)
    tile_area = jax.vmap(lambda own, number: routed_block(jax.random.fold_in(seeds[3], 2), own, number, TILE_SLOTS, N_AREA, 1, CAPACITY, 2))(tile_area_keys, tile_area_turns).reshape((TILES, 1))
    tile_block = with_ends(jax.random.randint(seeds[4], (TILES,), 0, COL_BLOCKS), jax.random.fold_in(seeds[4], 1), 0, COL_BLOCKS - 1).astype(jnp.int32)
    tile_row = with_ends(jax.random.randint(seeds[5], (TILES,), 0, ROW_BLOCKS), jax.random.fold_in(seeds[5], 1), 0, ROW_BLOCKS - 1).astype(jnp.int32)
    unit_bus = with_ends(jax.random.randint(seeds[6], (UNITS,), 0, BUS_AREA), jax.random.fold_in(seeds[6], 1), 0, BUS_AREA - 1).astype(jnp.int32)
    unit_class = with_ends(jax.random.randint(seeds[7], (UNITS,), 0, CLASSES), jax.random.fold_in(seeds[7], 1), 0, CLASSES - 1).astype(jnp.int32)
    power_cap = jnp.clip(jnp.exp(math.log(2.0) - 2.9957323 * jax.random.uniform(seeds[8], (UNITS,), jnp.float32) ** steps_of(seeds[8], (UNITS,), ((0, 8),), -0.2, 0.2)), 0.1, 2.0)
    line_limit = jnp.clip(jnp.exp(math.log(2.0) - 2.3025851 * jax.random.uniform(seeds[9], (LINES,), jnp.float32) ** steps_of(seeds[9], (LINES,), ((0, 8),), -0.2, 0.2)), 0.2, 2.0)
    smoother = draw_smoother(jax.random.fold_in(seeds[11], 71), 0)
    return {"demand": demand, "unit_cost": unit_cost, "ptdf_tiles": ptdf_tiles, "tile_area": tile_area, "tile_block": tile_block, "tile_row": tile_row, "unit_bus": unit_bus, "unit_class": unit_class, "power_cap": power_cap, "line_limit": line_limit, "smoother": smoother}


step_size = 0.5
rho_weight = 1.0

def reference(demand, unit_cost, ptdf_tiles, tile_area, tile_block, tile_row, unit_bus, unit_class, power_cap, line_limit, smoother):
    unit_total = unit_cost.shape[1]
    tile_total = ptdf_tiles.shape[0]
    line_total = line_limit.shape[0]
    bus_total = demand.shape[1]
    unit_buses = jnp.arange(unit_total, dtype=jnp.int32) // UNIT_AREA * BUS_AREA + unit_bus
    holder = jnp.arange(tile_total, dtype=jnp.int32) // TILE_SLOTS
    tile_columns = tile_area[:, 0] * COL_BLOCKS + tile_block
    tile_lines = holder * ROW_BLOCKS + tile_row
    tile_values = ptdf_tiles.astype(jnp.float32)
    kernel_spectrum = jnp.fft.rfft(smoother, axis=1)
    unit_spectrum = jnp.take(kernel_spectrum, unit_class, axis=0).T
    power = jnp.zeros((HORIZON, unit_total), jnp.float32)
    line_duals = jnp.zeros((HORIZON, line_total), jnp.float32)
    residuals = []
    for repeat in range(ITERATIONS):
        injection = demand.at[:, unit_buses].add(power).astype(jnp.bfloat16)
        panels = jnp.take(injection.reshape(HORIZON, N_AREA * COL_BLOCKS, PANEL_WIDTH), tile_columns, axis=1).astype(jnp.float32)
        partial_value = jnp.einsum('tjb,jlb->tjl', panels, tile_values)
        summed = jax.ops.segment_sum(jnp.moveaxis(partial_value, 1, 0), tile_lines, num_segments=N_AREA * ROW_BLOCKS)
        flows = jnp.moveaxis(summed, 0, 1).reshape(HORIZON, line_total)
        limits = line_limit[None, :]
        clipped = jnp.clip(flows + line_duals, -limits, limits)
        line_duals = line_duals + flows - clipped
        excess = flows - clipped
        residuals.append(jnp.sqrt(jnp.sum(excess * excess) / (HORIZON * line_total)))
        weights = (line_duals + flows - clipped).astype(jnp.bfloat16)
        picked = jnp.take(weights.reshape(HORIZON, N_AREA * ROW_BLOCKS, LINE_BLOCK), tile_lines, axis=1).astype(jnp.float32)
        contrib = jnp.einsum('tjl,jlb->tjb', picked, tile_values)
        gathered = jax.ops.segment_sum(jnp.moveaxis(contrib, 1, 0), tile_columns, num_segments=N_AREA * COL_BLOCKS)
        prices = jnp.moveaxis(gathered, 0, 1).reshape(HORIZON, bus_total)
        gradient = unit_cost + rho_weight * jnp.take(prices, unit_buses, axis=1)
        target = power - step_size * gradient
        smoothed = jnp.fft.irfft(jnp.fft.rfft(target, axis=0) * unit_spectrum, n=HORIZON, axis=0)
        power = jnp.clip(smoothed, -power_cap[None, :], power_cap[None, :])
    return (power, line_duals, jnp.stack(residuals))
```

```python
import functools
import math

import jax
import jax.numpy as jnp
from jax import lax
from jax.sharding import Mesh
from jax.sharding import PartitionSpec as P

ITERATIONS = 2
TM = ("tm_0", "tm_1")
AREA = ("area_0", "area_1")
TM_AREA = ("tm_0", "tm_1", "area_0", "area_1")


step_size = 0.5
rho_weight = 1.0


def laid_out(tiles, dim):
    dims = list(tiles.shape[1:])
    dims[dim] *= tiles.shape[0]
    return jnp.moveaxis(tiles, 0, dim).reshape(dims)


def copy_for_each(array, axis):
    count = lax.axis_size(axis)
    return lax.all_to_all(
        jnp.broadcast_to(array[None], (count, *array.shape)), axis, 0, 0, tiled=True
    )


def collect(array, axis, dim):
    return laid_out(copy_for_each(array, axis), dim)


def one_axis_at_a_time(array, axes):
    return functools.reduce(lax.psum, axes, array)


def per_device(
    demand,
    unit_cost,
    ptdf_tiles,
    tile_area,
    tile_block,
    tile_row,
    unit_bus,
    unit_class,
    power_cap,
    line_limit,
    smoother,
):
    time_devices = lax.axis_size(TM)
    area_devices = lax.axis_size(AREA)
    block_steps, bus_area = demand.shape
    unit_area = unit_cost.shape[1]
    tile_count, line_block, panel_width = ptdf_tiles.shape
    col_blocks = bus_area // panel_width
    row_blocks = line_limit.shape[0] // line_block
    capacity = 2 * tile_count // area_devices
    horizon = block_steps * time_devices
    unit_width = unit_area // time_devices
    area_index = lax.axis_index(AREA)
    time_index = lax.axis_index(TM)
    tile_areas = tile_area.reshape(area_devices, tile_count)
    block_grid = tile_block.reshape(area_devices, tile_count)
    row_grid = tile_row.reshape(area_devices, tile_count)
    is_source = (tile_areas == area_index).astype(jnp.int32)
    rank_source = jnp.cumsum(is_source, axis=1) - 1
    slot_ids = jnp.arange(capacity, dtype=jnp.int32)
    chosen = is_source[:, None, :] * (rank_source[:, None, :] == slot_ids[None, :, None]).astype(
        jnp.int32
    )
    send_block = jnp.sum(chosen * block_grid[:, None, :], axis=2).reshape(-1)
    my_areas = lax.dynamic_index_in_dim(tile_areas, area_index, 0, keepdims=False)
    my_blocks = lax.dynamic_index_in_dim(block_grid, area_index, 0, keepdims=False)
    my_rows = lax.dynamic_index_in_dim(row_grid, area_index, 0, keepdims=False)
    positions = jnp.arange(tile_count, dtype=jnp.int32)
    earlier = positions[None, :] <= positions[:, None]
    same_area = my_areas[None, :] == my_areas[:, None]
    rank_mine = jnp.sum((same_area & earlier).astype(jnp.int32), axis=1) - 1
    slot_of_tile = my_areas * capacity + rank_mine
    my_columns = my_areas * col_blocks + my_blocks
    my_class = lax.dynamic_slice_in_dim(unit_class, time_index * unit_width, unit_width)
    my_cap = lax.dynamic_slice_in_dim(power_cap, time_index * unit_width, unit_width)
    half_steps = horizon // 2
    steps_line = jnp.arange(horizon, dtype=jnp.int32)
    frequency = jnp.concatenate(
        [jnp.arange(half_steps + 1, dtype=jnp.int32), jnp.arange(1, half_steps, dtype=jnp.int32)]
    )
    angle = (frequency[:, None] * steps_line[None, :] % horizon).astype(jnp.float32) * (
        2.0 * math.pi / horizon
    )
    cosine_rows = (steps_line <= half_steps)[:, None]
    forward = jnp.where(cosine_rows, jnp.cos(angle), -jnp.sin(angle))
    edge_rows = (frequency == 0) | (frequency == half_steps)
    row_weight = (jnp.where(edge_rows, 1.0, 2.0).astype(jnp.float32) / horizon)[:, None]
    kernel_spectrum = jnp.dot(
        forward, smoother.T, precision=lax.Precision.HIGHEST, preferred_element_type=jnp.float32
    )
    class_table = (
        my_class[None, :] == jnp.arange(smoother.shape[0], dtype=jnp.int32)[:, None]
    ).astype(jnp.float32)
    unit_spectrum = jnp.dot(
        kernel_spectrum,
        class_table,
        precision=lax.Precision.HIGHEST,
        preferred_element_type=jnp.float32,
    )
    empty_row = jnp.zeros((1, unit_width), jnp.float32)
    kernel_real = unit_spectrum[: half_steps + 1]
    kernel_imag = jnp.concatenate([empty_row, unit_spectrum[half_steps + 1 :], empty_row], axis=0)
    power_time = jnp.zeros((block_steps, unit_area), jnp.float32)
    line_duals = jnp.zeros((block_steps, line_limit.shape[0]), jnp.float32)
    totals = []
    for repeat in range(ITERATIONS):
        if repeat == 0:
            injection = demand.astype(jnp.bfloat16)
        else:
            injection = demand.at[:, unit_bus].add(power_time).astype(jnp.bfloat16)
        gathered = collect(injection, AREA, 1)
        panels = jnp.take(
            gathered.reshape(block_steps, area_devices * col_blocks, panel_width),
            my_columns,
            axis=1,
        )
        partial_value = jnp.einsum(
            "tjb,jlb->tjl", panels, ptdf_tiles, preferred_element_type=jnp.float32
        )
        line_flows = (
            jnp.zeros((block_steps, row_blocks, line_block), jnp.float32)
            .at[:, my_rows]
            .add(partial_value)
        )
        line_flows = line_flows.reshape(block_steps, row_blocks * line_block)
        limits = line_limit[None, :]
        clipped = jnp.clip(line_flows + line_duals, -limits, limits)
        line_duals = line_duals + line_flows - clipped
        excess = line_flows - clipped
        local_total = jnp.sum(excess * excess)
        totals.append(local_total)
        weights = (line_duals + line_flows - clipped).astype(jnp.bfloat16)
        picked = jnp.take(weights.reshape(block_steps, row_blocks, line_block), my_rows, axis=1)
        contrib = jnp.einsum("tjl,jlb->tjb", picked, ptdf_tiles, preferred_element_type=jnp.float32)
        outbound = (
            jnp.zeros((block_steps, area_devices * capacity, panel_width), jnp.float32)
            .at[:, slot_of_tile]
            .set(contrib)
        )
        outbound = outbound.reshape(block_steps, area_devices, capacity, panel_width)
        returned = lax.all_to_all(outbound, AREA, split_axis=1, concat_axis=1, tiled=True)
        prices = (
            jnp.zeros((block_steps, col_blocks, panel_width), jnp.float32)
            .at[:, send_block]
            .add(returned.reshape(block_steps, area_devices * capacity, panel_width))
        )
        prices = prices.reshape(block_steps, bus_area)
        gradient = unit_cost + rho_weight * jnp.take(prices, unit_bus, axis=1)
        target = power_time - step_size * gradient
        columns = lax.all_to_all(target, TM, split_axis=1, concat_axis=0, tiled=True)
        spectrum = jnp.dot(
            forward, columns, precision=lax.Precision.HIGHEST, preferred_element_type=jnp.float32
        )
        spectrum_real = spectrum[: half_steps + 1]
        spectrum_imag = jnp.concatenate([empty_row, spectrum[half_steps + 1 :], empty_row], axis=0)
        product_real = spectrum_real * kernel_real - spectrum_imag * kernel_imag
        product_imag = spectrum_real * kernel_imag + spectrum_imag * kernel_real
        stacked = jnp.concatenate([product_real, product_imag[1:half_steps]], axis=0) * row_weight
        smoothed = lax.dot_general(
            forward,
            stacked,
            (((0,), (0,)), ((), ())),
            precision=lax.Precision.HIGHEST,
            preferred_element_type=jnp.float32,
        )
        power_cols = jnp.clip(smoothed, -my_cap[None, :], my_cap[None, :])
        power_time = lax.all_to_all(power_cols, TM, split_axis=0, concat_axis=1, tiled=True)
    entries = float(horizon * line_limit.shape[0] * area_devices)
    summed = lax.psum(jnp.stack(totals), TM_AREA)
    primal_rms = jnp.sqrt(summed / entries)
    return (power_time, line_duals, primal_rms)


def solution(mesh):
    finer = Mesh(mesh.devices.reshape(16, 4, 4, 2), ("tm_0", "tm_1", "area_0", "area_1"))
    placed = (
        P(TM, AREA),
        P(TM, AREA),
        P(AREA, None, None),
        P(),
        P(),
        P(),
        P(AREA),
        P(AREA),
        P(AREA),
        P(AREA),
        P(),
    )
    return jax.shard_map(
        per_device,
        mesh=finer,
        in_specs=placed,
        out_specs=(P(TM, AREA), P(TM, AREA), P()),
        check_vma=False,
    )
```

```python
import functools
import math

import jax
import jax.numpy as jnp
from jax import lax
from jax.sharding import Mesh
from jax.sharding import PartitionSpec as P
from jax.experimental import pallas as pl

ITERATIONS = 2
TM = ("tm_0", "tm_1")
AREA = ("area_0", "area_1")
TM_AREA = ("tm_0", "tm_1", "area_0", "area_1")


step_size = 0.5
rho_weight = 1.0


def laid_out(tiles, dim):
    dims = list(tiles.shape[1:])
    dims[dim] *= tiles.shape[0]
    return jnp.moveaxis(tiles, 0, dim).reshape(dims)


def copy_for_each(array, axis):
    count = lax.axis_size(axis)
    return lax.all_to_all(
        jnp.broadcast_to(array[None], (count, *array.shape)), axis, 0, 0, tiled=True
    )


def collect(array, axis, dim):
    return laid_out(copy_for_each(array, axis), dim)


PARTS = 3
ROWS = 16
UNIT_BLOCK = 1024


def split_parts(values):
    pieces = []
    rest = values
    for _ in range(PARTS):
        piece = rest.astype(jnp.bfloat16)
        pieces.append(piece)
        rest = rest - piece.astype(jnp.float32)
    return pieces


def gather_kernel(table_ref, lo_ref, hi_ref, out_ref):
    lanes = table_ref.shape[1]
    width = lo_ref.shape[1]
    onehot = (lax.broadcasted_iota(jnp.int32, (lanes, width), 0) == lo_ref[...]).astype(jnp.bfloat16)
    picked = jnp.dot(table_ref[...], onehot, preferred_element_type=jnp.float32)
    hi = hi_ref[...]
    total = jnp.zeros((ROWS, width), jnp.float32)
    for block in range(table_ref.shape[0] // ROWS):
        total = total + jnp.where(hi == block, picked[block * ROWS : (block + 1) * ROWS], 0.0)
    out_ref[...] = total


def bus_to_units(prices, lo_row, hi_row):
    steps, buses = prices.shape
    panel = 256
    blocks = buses // panel
    units = lo_row.shape[1]
    pieces = split_parts(prices.reshape(steps, blocks, panel))
    stacked = jnp.stack(pieces, axis=1).reshape(steps * PARTS, blocks, panel)
    stacked = jnp.pad(stacked, ((0, ROWS - steps * PARTS), (0, 0), (0, 0)))
    table = jnp.transpose(stacked, (1, 0, 2)).reshape(blocks * ROWS, panel)
    picked = pl.pallas_call(
        gather_kernel,
        grid=(units // UNIT_BLOCK,),
        in_specs=[
            pl.BlockSpec((blocks * ROWS, panel), lambda i: (0, 0)),
            pl.BlockSpec((1, UNIT_BLOCK), lambda i: (0, i)),
            pl.BlockSpec((1, UNIT_BLOCK), lambda i: (0, i)),
        ],
        out_specs=pl.BlockSpec((ROWS, UNIT_BLOCK), lambda i: (0, i)),
        out_shape=jax.ShapeDtypeStruct((ROWS, units), jnp.float32),
    )(table, lo_row, hi_row)
    parts = picked[: steps * PARTS].reshape(steps, PARTS, units)
    return parts[:, 0] + parts[:, 1] + parts[:, 2]


def scatter_kernel(parts_ref, lo_ref, hi_ref, out_ref):
    @pl.when(pl.program_id(0) == 0)
    def _():
        out_ref[...] = jnp.zeros(out_ref.shape, out_ref.dtype)

    width = parts_ref.shape[1]
    lanes = out_ref.shape[1]
    onehot = (lax.broadcasted_iota(jnp.int32, (width, lanes), 1) == lo_ref[...]).astype(jnp.bfloat16)
    parts = parts_ref[...]
    hi = hi_ref[...]
    masked = jnp.concatenate(
        [jnp.where(hi == block, parts, jnp.zeros_like(parts)) for block in range(out_ref.shape[0] // ROWS)],
        axis=0,
    )
    out_ref[...] += jnp.dot(masked, onehot, preferred_element_type=jnp.float32)


def units_to_bus(power, lo_col, hi_row, blocks, panel):
    steps, units = power.shape
    pieces = split_parts(power)
    parts = jnp.concatenate(pieces + [jnp.zeros((ROWS - steps * PARTS, units), jnp.bfloat16)], axis=0)
    summed = pl.pallas_call(
        scatter_kernel,
        grid=(units // UNIT_BLOCK,),
        in_specs=[
            pl.BlockSpec((ROWS, UNIT_BLOCK), lambda i: (0, i)),
            pl.BlockSpec((UNIT_BLOCK, 1), lambda i: (i, 0)),
            pl.BlockSpec((1, UNIT_BLOCK), lambda i: (0, i)),
        ],
        out_specs=pl.BlockSpec((blocks * ROWS, panel), lambda i: (0, 0)),
        out_shape=jax.ShapeDtypeStruct((blocks * ROWS, panel), jnp.float32),
    )(parts, lo_col, hi_row)
    summed = summed.reshape(blocks, ROWS, panel)[:, : steps * PARTS].reshape(blocks, PARTS, steps, panel)
    summed = summed[:, 0] + summed[:, 1] + summed[:, 2]
    return jnp.transpose(summed, (1, 0, 2)).reshape(steps, blocks * panel)


def one_axis_at_a_time(array, axes):
    return functools.reduce(lax.psum, axes, array)


def per_device(
    demand,
    unit_cost,
    ptdf_tiles,
    tile_area,
    tile_block,
    tile_row,
    unit_bus,
    unit_class,
    power_cap,
    line_limit,
    smoother,
):
    time_devices = lax.axis_size(TM)
    area_devices = lax.axis_size(AREA)
    block_steps, bus_area = demand.shape
    unit_area = unit_cost.shape[1]
    tile_count, line_block, panel_width = ptdf_tiles.shape
    col_blocks = bus_area // panel_width
    row_blocks = line_limit.shape[0] // line_block
    capacity = 2 * tile_count // area_devices
    horizon = block_steps * time_devices
    unit_width = unit_area // time_devices
    area_index = lax.axis_index(AREA)
    time_index = lax.axis_index(TM)
    tile_areas = tile_area.reshape(area_devices, tile_count)
    block_grid = tile_block.reshape(area_devices, tile_count)
    row_grid = tile_row.reshape(area_devices, tile_count)
    is_source = (tile_areas == area_index).astype(jnp.int32)
    rank_source = jnp.cumsum(is_source, axis=1) - 1
    slot_ids = jnp.arange(capacity, dtype=jnp.int32)
    chosen = is_source[:, None, :] * (rank_source[:, None, :] == slot_ids[None, :, None]).astype(
        jnp.int32
    )
    send_block = jnp.sum(chosen * block_grid[:, None, :], axis=2).reshape(-1)
    my_areas = lax.dynamic_index_in_dim(tile_areas, area_index, 0, keepdims=False)
    my_blocks = lax.dynamic_index_in_dim(block_grid, area_index, 0, keepdims=False)
    my_rows = lax.dynamic_index_in_dim(row_grid, area_index, 0, keepdims=False)
    positions = jnp.arange(tile_count, dtype=jnp.int32)
    earlier = positions[None, :] <= positions[:, None]
    same_area = my_areas[None, :] == my_areas[:, None]
    rank_mine = jnp.sum((same_area & earlier).astype(jnp.int32), axis=1) - 1
    slot_of_tile = my_areas * capacity + rank_mine
    my_columns = my_areas * col_blocks + my_blocks
    my_class = lax.dynamic_slice_in_dim(unit_class, time_index * unit_width, unit_width)
    my_cap = lax.dynamic_slice_in_dim(power_cap, time_index * unit_width, unit_width)
    half_steps = horizon // 2
    steps_line = jnp.arange(horizon, dtype=jnp.int32)
    frequency = jnp.concatenate(
        [jnp.arange(half_steps + 1, dtype=jnp.int32), jnp.arange(1, half_steps, dtype=jnp.int32)]
    )
    angle = (frequency[:, None] * steps_line[None, :] % horizon).astype(jnp.float32) * (
        2.0 * math.pi / horizon
    )
    cosine_rows = (steps_line <= half_steps)[:, None]
    forward = jnp.where(cosine_rows, jnp.cos(angle), -jnp.sin(angle))
    edge_rows = (frequency == 0) | (frequency == half_steps)
    row_weight = (jnp.where(edge_rows, 1.0, 2.0).astype(jnp.float32) / horizon)[:, None]
    kernel_spectrum = jnp.dot(
        forward, smoother.T, precision=lax.Precision.HIGHEST, preferred_element_type=jnp.float32
    )
    class_table = (
        my_class[None, :] == jnp.arange(smoother.shape[0], dtype=jnp.int32)[:, None]
    ).astype(jnp.float32)
    unit_spectrum = jnp.dot(
        kernel_spectrum,
        class_table,
        precision=lax.Precision.HIGHEST,
        preferred_element_type=jnp.float32,
    )
    empty_row = jnp.zeros((1, unit_width), jnp.float32)
    kernel_real = unit_spectrum[: half_steps + 1]
    kernel_imag = jnp.concatenate([empty_row, unit_spectrum[half_steps + 1 :], empty_row], axis=0)
    lo_row = (unit_bus % panel_width).reshape(1, unit_area)
    hi_row = (unit_bus // panel_width).reshape(1, unit_area)
    lo_col = lo_row.reshape(unit_area, 1)
    power_time = jnp.zeros((block_steps, unit_area), jnp.float32)
    line_duals = jnp.zeros((block_steps, line_limit.shape[0]), jnp.float32)
    totals = []
    for repeat in range(ITERATIONS):
        if repeat == 0:
            injection = demand.astype(jnp.bfloat16)
        else:
            injection = (demand + units_to_bus(power_time, lo_col, hi_row, col_blocks, panel_width)).astype(
                jnp.bfloat16
            )
        gathered = collect(injection, AREA, 1)
        panels = jnp.take(
            gathered.reshape(block_steps, area_devices * col_blocks, panel_width),
            my_columns,
            axis=1,
        )
        partial_value = jnp.einsum(
            "tjb,jlb->tjl", panels, ptdf_tiles, preferred_element_type=jnp.float32
        )
        line_flows = (
            jnp.zeros((block_steps, row_blocks, line_block), jnp.float32)
            .at[:, my_rows]
            .add(partial_value)
        )
        line_flows = line_flows.reshape(block_steps, row_blocks * line_block)
        limits = line_limit[None, :]
        clipped = jnp.clip(line_flows + line_duals, -limits, limits)
        line_duals = line_duals + line_flows - clipped
        excess = line_flows - clipped
        local_total = jnp.sum(excess * excess)
        totals.append(local_total)
        weights = (line_duals + line_flows - clipped).astype(jnp.bfloat16)
        picked = jnp.take(weights.reshape(block_steps, row_blocks, line_block), my_rows, axis=1)
        contrib = jnp.einsum("tjl,jlb->tjb", picked, ptdf_tiles, preferred_element_type=jnp.float32)
        outbound = (
            jnp.zeros((block_steps, area_devices * capacity, panel_width), jnp.float32)
            .at[:, slot_of_tile]
            .set(contrib)
        )
        outbound = outbound.reshape(block_steps, area_devices, capacity, panel_width)
        last = repeat == ITERATIONS - 1
        if last:
            extra = (
                jnp.zeros((block_steps, area_devices, 1, panel_width), jnp.float32)
                .at[0, :, 0, :ITERATIONS]
                .set(jnp.broadcast_to(jnp.stack(totals), (area_devices, ITERATIONS)))
            )
            outbound = jnp.concatenate([outbound, extra], axis=2)
        returned = lax.all_to_all(outbound, AREA, split_axis=1, concat_axis=1, tiled=True)
        if last:
            area_totals = jnp.sum(returned[0, :, capacity, :ITERATIONS], axis=0)
            returned = returned[:, :, :capacity]
        prices = (
            jnp.zeros((block_steps, col_blocks, panel_width), jnp.float32)
            .at[:, send_block]
            .add(returned.reshape(block_steps, area_devices * capacity, panel_width))
        )
        prices = prices.reshape(block_steps, bus_area)
        gradient = unit_cost + rho_weight * bus_to_units(prices, lo_row, hi_row)
        target = power_time - step_size * gradient
        columns = lax.all_to_all(target, TM, split_axis=1, concat_axis=0, tiled=True)
        spectrum = jnp.dot(
            forward, columns, precision=lax.Precision.HIGHEST, preferred_element_type=jnp.float32
        )
        spectrum_real = spectrum[: half_steps + 1]
        spectrum_imag = jnp.concatenate([empty_row, spectrum[half_steps + 1 :], empty_row], axis=0)
        product_real = spectrum_real * kernel_real - spectrum_imag * kernel_imag
        product_imag = spectrum_real * kernel_imag + spectrum_imag * kernel_real
        stacked = jnp.concatenate([product_real, product_imag[1:half_steps]], axis=0) * row_weight
        smoothed = lax.dot_general(
            forward,
            stacked,
            (((0,), (0,)), ((), ())),
            precision=lax.Precision.HIGHEST,
            preferred_element_type=jnp.float32,
        )
        power_cols = jnp.clip(smoothed, -my_cap[None, :], my_cap[None, :])
        if last:
            chunks = power_cols.reshape(time_devices, block_steps, unit_width)
            extra = (
                jnp.zeros((time_devices, 1, unit_width), jnp.float32)
                .at[:, 0, :ITERATIONS]
                .set(jnp.broadcast_to(area_totals, (time_devices, ITERATIONS)))
            )
            received = lax.all_to_all(
                jnp.concatenate([chunks, extra], axis=1), TM, split_axis=0, concat_axis=0, tiled=True
            )
            summed = jnp.sum(received[:, block_steps, :ITERATIONS], axis=0)
            power_time = jnp.transpose(received[:, :block_steps], (1, 0, 2)).reshape(block_steps, unit_area)
        else:
            power_time = lax.all_to_all(power_cols, TM, split_axis=0, concat_axis=1, tiled=True)
    entries = float(horizon * line_limit.shape[0] * area_devices)
    primal_rms = jnp.sqrt(summed / entries)
    return (power_time, line_duals, primal_rms)


def solution(mesh):
    finer = Mesh(mesh.devices.reshape(16, 4, 4, 2), ("tm_0", "tm_1", "area_0", "area_1"))
    placed = (
        P(TM, AREA),
        P(TM, AREA),
        P(AREA, None, None),
        P(),
        P(),
        P(),
        P(AREA),
        P(AREA),
        P(AREA),
        P(AREA),
        P(),
    )
    return jax.shard_map(
        per_device,
        mesh=finer,
        in_specs=placed,
        out_specs=(P(TM, AREA), P(TM, AREA), P()),
        check_vma=False,
    )
```

```python
import functools
import math

import jax
import jax.numpy as jnp
from jax import lax
from jax.sharding import Mesh
from jax.sharding import PartitionSpec as P
from jax.experimental import pallas as pl

ITERATIONS = 2
TM = ("tm_0", "tm_1")
AREA = ("area_0", "area_1")
TM_AREA = ("tm_0", "tm_1", "area_0", "area_1")


step_size = 0.5
rho_weight = 1.0


def laid_out(tiles, dim):
    dims = list(tiles.shape[1:])
    dims[dim] *= tiles.shape[0]
    return jnp.moveaxis(tiles, 0, dim).reshape(dims)


def copy_for_each(array, axis):
    count = lax.axis_size(axis)
    return lax.all_to_all(
        jnp.broadcast_to(array[None], (count, *array.shape)), axis, 0, 0, tiled=True
    )


def collect(array, axis, dim):
    return laid_out(copy_for_each(array, axis), dim)


PARTS = 3
ROWS = 16
UNIT_BLOCK = 1024


def split_parts(values):
    pieces = []
    rest = values
    for _ in range(PARTS):
        piece = rest.astype(jnp.bfloat16)
        pieces.append(piece)
        rest = rest - piece.astype(jnp.float32)
    return pieces


def gather_kernel(table_ref, lo_ref, hi_ref, out_ref):
    lanes = table_ref.shape[1]
    width = lo_ref.shape[1]
    onehot = (lax.broadcasted_iota(jnp.int32, (lanes, width), 0) == lo_ref[...]).astype(jnp.bfloat16)
    picked = jnp.dot(table_ref[...], onehot, preferred_element_type=jnp.float32)
    hi = hi_ref[...]
    total = jnp.zeros((ROWS, width), jnp.float32)
    for block in range(table_ref.shape[0] // ROWS):
        total = total + jnp.where(hi == block, picked[block * ROWS : (block + 1) * ROWS], 0.0)
    out_ref[...] = total


def bus_to_units(prices, lo_row, hi_row):
    steps, buses = prices.shape
    panel = 256
    blocks = buses // panel
    units = lo_row.shape[1]
    pieces = split_parts(prices.reshape(steps, blocks, panel))
    stacked = jnp.stack(pieces, axis=1).reshape(steps * PARTS, blocks, panel)
    stacked = jnp.pad(stacked, ((0, ROWS - steps * PARTS), (0, 0), (0, 0)))
    table = jnp.transpose(stacked, (1, 0, 2)).reshape(blocks * ROWS, panel)
    picked = pl.pallas_call(
        gather_kernel,
        grid=(units // UNIT_BLOCK,),
        in_specs=[
            pl.BlockSpec((blocks * ROWS, panel), lambda i: (0, 0)),
            pl.BlockSpec((1, UNIT_BLOCK), lambda i: (0, i)),
            pl.BlockSpec((1, UNIT_BLOCK), lambda i: (0, i)),
        ],
        out_specs=pl.BlockSpec((ROWS, UNIT_BLOCK), lambda i: (0, i)),
        out_shape=jax.ShapeDtypeStruct((ROWS, units), jnp.float32),
    )(table, lo_row, hi_row)
    parts = picked[: steps * PARTS].reshape(steps, PARTS, units)
    return parts[:, 0] + parts[:, 1] + parts[:, 2]


def scatter_kernel(parts_ref, lo_ref, hi_ref, out_ref):
    @pl.when(pl.program_id(0) == 0)
    def _():
        out_ref[...] = jnp.zeros(out_ref.shape, out_ref.dtype)

    width = parts_ref.shape[1]
    lanes = out_ref.shape[1]
    onehot = (lax.broadcasted_iota(jnp.int32, (width, lanes), 1) == lo_ref[...]).astype(jnp.bfloat16)
    parts = parts_ref[...]
    hi = hi_ref[...]
    masked = jnp.concatenate(
        [jnp.where(hi == block, parts, jnp.zeros_like(parts)) for block in range(out_ref.shape[0] // ROWS)],
        axis=0,
    )
    out_ref[...] += jnp.dot(masked, onehot, preferred_element_type=jnp.float32)


def units_to_bus(power, lo_col, hi_row, blocks, panel):
    steps, units = power.shape
    pieces = split_parts(power)
    parts = jnp.concatenate(pieces + [jnp.zeros((ROWS - steps * PARTS, units), jnp.bfloat16)], axis=0)
    summed = pl.pallas_call(
        scatter_kernel,
        grid=(units // UNIT_BLOCK,),
        in_specs=[
            pl.BlockSpec((ROWS, UNIT_BLOCK), lambda i: (0, i)),
            pl.BlockSpec((UNIT_BLOCK, 1), lambda i: (i, 0)),
            pl.BlockSpec((1, UNIT_BLOCK), lambda i: (0, i)),
        ],
        out_specs=pl.BlockSpec((blocks * ROWS, panel), lambda i: (0, 0)),
        out_shape=jax.ShapeDtypeStruct((blocks * ROWS, panel), jnp.float32),
    )(parts, lo_col, hi_row)
    summed = summed.reshape(blocks, ROWS, panel)[:, : steps * PARTS].reshape(blocks, PARTS, steps, panel)
    summed = summed[:, 0] + summed[:, 1] + summed[:, 2]
    return jnp.transpose(summed, (1, 0, 2)).reshape(steps, blocks * panel)


def one_axis_at_a_time(array, axes):
    return functools.reduce(lax.psum, axes, array)


def per_device(
    demand,
    unit_cost,
    ptdf_tiles,
    tile_area,
    tile_block,
    tile_row,
    unit_bus,
    unit_class,
    power_cap,
    line_limit,
    smoother,
):
    time_devices = lax.axis_size(TM)
    area_devices = lax.axis_size(AREA)
    block_steps, bus_area = demand.shape
    unit_area = unit_cost.shape[1]
    tile_count, line_block, panel_width = ptdf_tiles.shape
    col_blocks = bus_area // panel_width
    row_blocks = line_limit.shape[0] // line_block
    capacity = 2 * tile_count // area_devices
    horizon = block_steps * time_devices
    unit_width = unit_area // time_devices
    area_index = lax.axis_index(AREA)
    time_index = lax.axis_index(TM)
    tile_areas = tile_area.reshape(area_devices, tile_count)
    block_grid = tile_block.reshape(area_devices, tile_count)
    row_grid = tile_row.reshape(area_devices, tile_count)
    is_source = (tile_areas == area_index).astype(jnp.int32)
    rank_source = jnp.cumsum(is_source, axis=1) - 1
    slot_ids = jnp.arange(capacity, dtype=jnp.int32)
    chosen = is_source[:, None, :] * (rank_source[:, None, :] == slot_ids[None, :, None]).astype(
        jnp.int32
    )
    send_block = jnp.sum(chosen * block_grid[:, None, :], axis=2).reshape(-1)
    my_areas = lax.dynamic_index_in_dim(tile_areas, area_index, 0, keepdims=False)
    my_blocks = lax.dynamic_index_in_dim(block_grid, area_index, 0, keepdims=False)
    my_rows = lax.dynamic_index_in_dim(row_grid, area_index, 0, keepdims=False)
    positions = jnp.arange(tile_count, dtype=jnp.int32)
    earlier = positions[None, :] <= positions[:, None]
    same_area = my_areas[None, :] == my_areas[:, None]
    rank_mine = jnp.sum((same_area & earlier).astype(jnp.int32), axis=1) - 1
    slot_of_tile = my_areas * capacity + rank_mine
    my_columns = my_areas * col_blocks + my_blocks
    my_class = lax.dynamic_slice_in_dim(unit_class, time_index * unit_width, unit_width)
    my_cap = lax.dynamic_slice_in_dim(power_cap, time_index * unit_width, unit_width)
    half_steps = horizon // 2
    steps_line = jnp.arange(horizon, dtype=jnp.int32)
    frequency = jnp.concatenate(
        [jnp.arange(half_steps + 1, dtype=jnp.int32), jnp.arange(1, half_steps, dtype=jnp.int32)]
    )
    angle = (frequency[:, None] * steps_line[None, :] % horizon).astype(jnp.float32) * (
        2.0 * math.pi / horizon
    )
    cosine_rows = (steps_line <= half_steps)[:, None]
    forward = jnp.where(cosine_rows, jnp.cos(angle), -jnp.sin(angle))
    edge_rows = (frequency == 0) | (frequency == half_steps)
    row_weight = (jnp.where(edge_rows, 1.0, 2.0).astype(jnp.float32) / horizon)[:, None]
    kernel_spectrum = jnp.dot(
        forward, smoother.T, precision=lax.Precision.HIGHEST, preferred_element_type=jnp.float32
    )
    class_table = (
        my_class[None, :] == jnp.arange(smoother.shape[0], dtype=jnp.int32)[:, None]
    ).astype(jnp.float32)
    unit_spectrum = jnp.dot(
        kernel_spectrum,
        class_table,
        precision=lax.Precision.HIGHEST,
        preferred_element_type=jnp.float32,
    )
    empty_row = jnp.zeros((1, unit_width), jnp.float32)
    kernel_real = unit_spectrum[: half_steps + 1]
    kernel_imag = jnp.concatenate([empty_row, unit_spectrum[half_steps + 1 :], empty_row], axis=0)
    lo_row = (unit_bus % panel_width).reshape(1, unit_area)
    hi_row = (unit_bus // panel_width).reshape(1, unit_area)
    lo_col = lo_row.reshape(unit_area, 1)
    power_time = jnp.zeros((block_steps, unit_area), jnp.float32)
    line_duals = jnp.zeros((block_steps, line_limit.shape[0]), jnp.float32)
    totals = []
    for repeat in range(ITERATIONS):
        if repeat == 0:
            injection = demand.astype(jnp.bfloat16)
        else:
            injection = (demand + units_to_bus(power_time, lo_col, hi_row, col_blocks, panel_width)).astype(
                jnp.bfloat16
            )
        sending = jnp.take(injection.reshape(block_steps, col_blocks, panel_width), send_block, axis=1)
        arrived = lax.all_to_all(
            sending.reshape(block_steps, area_devices, capacity, panel_width),
            AREA,
            split_axis=1,
            concat_axis=1,
            tiled=True,
        )
        panels = jnp.take(
            arrived.reshape(block_steps, area_devices * capacity, panel_width), slot_of_tile, axis=1
        )
        partial_value = jnp.einsum(
            "tjb,jlb->tjl", panels, ptdf_tiles, preferred_element_type=jnp.float32
        )
        line_flows = (
            jnp.zeros((block_steps, row_blocks, line_block), jnp.float32)
            .at[:, my_rows]
            .add(partial_value)
        )
        line_flows = line_flows.reshape(block_steps, row_blocks * line_block)
        limits = line_limit[None, :]
        clipped = jnp.clip(line_flows + line_duals, -limits, limits)
        line_duals = line_duals + line_flows - clipped
        excess = line_flows - clipped
        local_total = jnp.sum(excess * excess)
        totals.append(local_total)
        weights = (line_duals + line_flows - clipped).astype(jnp.bfloat16)
        picked = jnp.take(weights.reshape(block_steps, row_blocks, line_block), my_rows, axis=1)
        contrib = jnp.einsum("tjl,jlb->tjb", picked, ptdf_tiles, preferred_element_type=jnp.float32)
        outbound = (
            jnp.zeros((block_steps, area_devices * capacity, panel_width), jnp.float32)
            .at[:, slot_of_tile]
            .set(contrib)
        )
        outbound = outbound.reshape(block_steps, area_devices, capacity, panel_width)
        last = repeat == ITERATIONS - 1
        if last:
            extra = (
                jnp.zeros((block_steps, area_devices, 1, panel_width), jnp.float32)
                .at[0, :, 0, :ITERATIONS]
                .set(jnp.broadcast_to(jnp.stack(totals), (area_devices, ITERATIONS)))
            )
            outbound = jnp.concatenate([outbound, extra], axis=2)
        returned = lax.all_to_all(outbound, AREA, split_axis=1, concat_axis=1, tiled=True)
        if last:
            area_totals = jnp.sum(returned[0, :, capacity, :ITERATIONS], axis=0)
            returned = returned[:, :, :capacity]
        prices = (
            jnp.zeros((block_steps, col_blocks, panel_width), jnp.float32)
            .at[:, send_block]
            .add(returned.reshape(block_steps, area_devices * capacity, panel_width))
        )
        prices = prices.reshape(block_steps, bus_area)
        gradient = unit_cost + rho_weight * bus_to_units(prices, lo_row, hi_row)
        target = power_time - step_size * gradient
        columns = lax.all_to_all(target, TM, split_axis=1, concat_axis=0, tiled=True)
        spectrum = jnp.dot(
            forward, columns, precision=lax.Precision.HIGHEST, preferred_element_type=jnp.float32
        )
        spectrum_real = spectrum[: half_steps + 1]
        spectrum_imag = jnp.concatenate([empty_row, spectrum[half_steps + 1 :], empty_row], axis=0)
        product_real = spectrum_real * kernel_real - spectrum_imag * kernel_imag
        product_imag = spectrum_real * kernel_imag + spectrum_imag * kernel_real
        stacked = jnp.concatenate([product_real, product_imag[1:half_steps]], axis=0) * row_weight
        smoothed = lax.dot_general(
            forward,
            stacked,
            (((0,), (0,)), ((), ())),
            precision=lax.Precision.HIGHEST,
            preferred_element_type=jnp.float32,
        )
        power_cols = jnp.clip(smoothed, -my_cap[None, :], my_cap[None, :])
        if last:
            chunks = power_cols.reshape(time_devices, block_steps, unit_width)
            extra = (
                jnp.zeros((time_devices, 1, unit_width), jnp.float32)
                .at[:, 0, :ITERATIONS]
                .set(jnp.broadcast_to(area_totals, (time_devices, ITERATIONS)))
            )
            received = lax.all_to_all(
                jnp.concatenate([chunks, extra], axis=1), TM, split_axis=0, concat_axis=0, tiled=True
            )
            summed = jnp.sum(received[:, block_steps, :ITERATIONS], axis=0)
            power_time = jnp.transpose(received[:, :block_steps], (1, 0, 2)).reshape(block_steps, unit_area)
        else:
            power_time = lax.all_to_all(power_cols, TM, split_axis=0, concat_axis=1, tiled=True)
    entries = float(horizon * line_limit.shape[0] * area_devices)
    primal_rms = jnp.sqrt(summed / entries)
    return (power_time, line_duals, primal_rms)


def solution(mesh):
    finer = Mesh(mesh.devices.reshape(16, 4, 4, 2), ("tm_0", "tm_1", "area_0", "area_1"))
    placed = (
        P(TM, AREA),
        P(TM, AREA),
        P(AREA, None, None),
        P(),
        P(),
        P(),
        P(AREA),
        P(AREA),
        P(AREA),
        P(AREA),
        P(),
    )
    return jax.shard_map(
        per_device,
        mesh=finer,
        in_specs=placed,
        out_specs=(P(TM, AREA), P(TM, AREA), P()),
        check_vma=False,
    )
```

```python
import functools
import math

import jax
import jax.numpy as jnp
from jax import lax
from jax.sharding import Mesh
from jax.sharding import PartitionSpec as P
from jax.experimental import pallas as pl

ITERATIONS = 2
TM = ("tm_0", "tm_1")
AREA = ("area_0", "area_1")
TM_AREA = ("tm_0", "tm_1", "area_0", "area_1")


step_size = 0.5
rho_weight = 1.0


def laid_out(tiles, dim):
    dims = list(tiles.shape[1:])
    dims[dim] *= tiles.shape[0]
    return jnp.moveaxis(tiles, 0, dim).reshape(dims)


def copy_for_each(array, axis):
    count = lax.axis_size(axis)
    return lax.all_to_all(
        jnp.broadcast_to(array[None], (count, *array.shape)), axis, 0, 0, tiled=True
    )


def collect(array, axis, dim):
    return laid_out(copy_for_each(array, axis), dim)


PARTS = 3
ROWS = 16
UNIT_BLOCK = 1024


def split_parts(values):
    pieces = []
    rest = values
    for _ in range(PARTS):
        piece = rest.astype(jnp.bfloat16)
        pieces.append(piece)
        rest = rest - piece.astype(jnp.float32)
    return pieces


def gather_kernel(table_ref, lo_ref, hi_ref, out_ref):
    lanes = table_ref.shape[1]
    width = lo_ref.shape[1]
    onehot = (lax.broadcasted_iota(jnp.int32, (lanes, width), 0) == lo_ref[...]).astype(jnp.bfloat16)
    picked = jnp.dot(table_ref[...], onehot, preferred_element_type=jnp.float32)
    hi = hi_ref[...]
    total = jnp.zeros((ROWS, width), jnp.float32)
    for block in range(table_ref.shape[0] // ROWS):
        total = total + jnp.where(hi == block, picked[block * ROWS : (block + 1) * ROWS], 0.0)
    out_ref[...] = total


def bus_to_units(prices, lo_row, hi_row):
    steps, buses = prices.shape
    panel = 256
    blocks = buses // panel
    units = lo_row.shape[1]
    pieces = split_parts(prices.reshape(steps, blocks, panel))
    stacked = jnp.stack(pieces, axis=1).reshape(steps * PARTS, blocks, panel)
    stacked = jnp.pad(stacked, ((0, ROWS - steps * PARTS), (0, 0), (0, 0)))
    table = jnp.transpose(stacked, (1, 0, 2)).reshape(blocks * ROWS, panel)
    picked = pl.pallas_call(
        gather_kernel,
        grid=(units // UNIT_BLOCK,),
        in_specs=[
            pl.BlockSpec((blocks * ROWS, panel), lambda i: (0, 0)),
            pl.BlockSpec((1, UNIT_BLOCK), lambda i: (0, i)),
            pl.BlockSpec((1, UNIT_BLOCK), lambda i: (0, i)),
        ],
        out_specs=pl.BlockSpec((ROWS, UNIT_BLOCK), lambda i: (0, i)),
        out_shape=jax.ShapeDtypeStruct((ROWS, units), jnp.float32),
    )(table, lo_row, hi_row)
    parts = picked[: steps * PARTS].reshape(steps, PARTS, units)
    return parts[:, 0] + parts[:, 1] + parts[:, 2]


def scatter_kernel(parts_ref, lo_ref, hi_ref, out_ref):
    @pl.when(pl.program_id(0) == 0)
    def _():
        out_ref[...] = jnp.zeros(out_ref.shape, out_ref.dtype)

    width = parts_ref.shape[1]
    lanes = out_ref.shape[1]
    onehot = (lax.broadcasted_iota(jnp.int32, (width, lanes), 1) == lo_ref[...]).astype(jnp.bfloat16)
    parts = parts_ref[...]
    hi = hi_ref[...]
    masked = jnp.concatenate(
        [jnp.where(hi == block, parts, jnp.zeros_like(parts)) for block in range(out_ref.shape[0] // ROWS)],
        axis=0,
    )
    out_ref[...] += jnp.dot(masked, onehot, preferred_element_type=jnp.float32)


def units_to_bus(power, lo_col, hi_row, blocks, panel):
    steps, units = power.shape
    pieces = split_parts(power)
    parts = jnp.concatenate(pieces + [jnp.zeros((ROWS - steps * PARTS, units), jnp.bfloat16)], axis=0)
    summed = pl.pallas_call(
        scatter_kernel,
        grid=(units // UNIT_BLOCK,),
        in_specs=[
            pl.BlockSpec((ROWS, UNIT_BLOCK), lambda i: (0, i)),
            pl.BlockSpec((UNIT_BLOCK, 1), lambda i: (i, 0)),
            pl.BlockSpec((1, UNIT_BLOCK), lambda i: (0, i)),
        ],
        out_specs=pl.BlockSpec((blocks * ROWS, panel), lambda i: (0, 0)),
        out_shape=jax.ShapeDtypeStruct((blocks * ROWS, panel), jnp.float32),
    )(parts, lo_col, hi_row)
    summed = summed.reshape(blocks, ROWS, panel)[:, : steps * PARTS].reshape(blocks, PARTS, steps, panel)
    summed = summed[:, 0] + summed[:, 1] + summed[:, 2]
    return jnp.transpose(summed, (1, 0, 2)).reshape(steps, blocks * panel)


def one_axis_at_a_time(array, axes):
    return functools.reduce(lax.psum, axes, array)


def per_device(
    demand,
    unit_cost,
    ptdf_tiles,
    tile_area,
    tile_block,
    tile_row,
    unit_bus,
    unit_class,
    power_cap,
    line_limit,
    smoother,
):
    time_devices = lax.axis_size(TM)
    area_devices = lax.axis_size(AREA)
    block_steps, bus_area = demand.shape
    unit_area = unit_cost.shape[1]
    tile_count, line_block, panel_width = ptdf_tiles.shape
    col_blocks = bus_area // panel_width
    row_blocks = line_limit.shape[0] // line_block
    capacity = 2 * tile_count // area_devices
    horizon = block_steps * time_devices
    unit_width = unit_area // time_devices
    area_index = lax.axis_index(AREA)
    time_index = lax.axis_index(TM)
    tile_areas = tile_area.reshape(area_devices, tile_count)
    block_grid = tile_block.reshape(area_devices, tile_count)
    row_grid = tile_row.reshape(area_devices, tile_count)
    is_source = (tile_areas == area_index).astype(jnp.int32)
    rank_source = jnp.cumsum(is_source, axis=1) - 1
    slot_ids = jnp.arange(capacity, dtype=jnp.int32)
    chosen = is_source[:, None, :] * (rank_source[:, None, :] == slot_ids[None, :, None]).astype(
        jnp.int32
    )
    send_block = jnp.sum(chosen * block_grid[:, None, :], axis=2).reshape(-1)
    my_areas = lax.dynamic_index_in_dim(tile_areas, area_index, 0, keepdims=False)
    my_blocks = lax.dynamic_index_in_dim(block_grid, area_index, 0, keepdims=False)
    my_rows = lax.dynamic_index_in_dim(row_grid, area_index, 0, keepdims=False)
    positions = jnp.arange(tile_count, dtype=jnp.int32)
    earlier = positions[None, :] <= positions[:, None]
    same_area = my_areas[None, :] == my_areas[:, None]
    rank_mine = jnp.sum((same_area & earlier).astype(jnp.int32), axis=1) - 1
    slot_of_tile = my_areas * capacity + rank_mine
    my_columns = my_areas * col_blocks + my_blocks
    my_class = lax.dynamic_slice_in_dim(unit_class, time_index * unit_width, unit_width)
    my_cap = lax.dynamic_slice_in_dim(power_cap, time_index * unit_width, unit_width)
    half_steps = horizon // 2
    steps_line = jnp.arange(horizon, dtype=jnp.int32)
    frequency = jnp.concatenate(
        [jnp.arange(half_steps + 1, dtype=jnp.int32), jnp.arange(1, half_steps, dtype=jnp.int32)]
    )
    angle = (frequency[:, None] * steps_line[None, :] % horizon).astype(jnp.float32) * (
        2.0 * math.pi / horizon
    )
    cosine_rows = (steps_line <= half_steps)[:, None]
    forward = jnp.where(cosine_rows, jnp.cos(angle), -jnp.sin(angle))
    edge_rows = (frequency == 0) | (frequency == half_steps)
    row_weight = (jnp.where(edge_rows, 1.0, 2.0).astype(jnp.float32) / horizon)[:, None]
    kernel_spectrum = jnp.dot(
        forward, smoother.T, precision=lax.Precision.HIGHEST, preferred_element_type=jnp.float32
    )
    class_table = (
        my_class[None, :] == jnp.arange(smoother.shape[0], dtype=jnp.int32)[:, None]
    ).astype(jnp.float32)
    unit_spectrum = jnp.dot(
        kernel_spectrum,
        class_table,
        precision=lax.Precision.HIGHEST,
        preferred_element_type=jnp.float32,
    )
    empty_row = jnp.zeros((1, unit_width), jnp.float32)
    kernel_real = unit_spectrum[: half_steps + 1]
    kernel_imag = jnp.concatenate([empty_row, unit_spectrum[half_steps + 1 :], empty_row], axis=0)
    row_table = (my_rows[:, None] == jnp.arange(row_blocks, dtype=jnp.int32)[None, :]).astype(jnp.float32)
    slot_table = (
        slot_of_tile[:, None] == jnp.arange(area_devices * capacity, dtype=jnp.int32)[None, :]
    ).astype(jnp.float32)
    block_table = (send_block[:, None] == jnp.arange(col_blocks, dtype=jnp.int32)[None, :]).astype(jnp.float32)
    lo_row = (unit_bus % panel_width).reshape(1, unit_area)
    hi_row = (unit_bus // panel_width).reshape(1, unit_area)
    lo_col = lo_row.reshape(unit_area, 1)
    power_time = jnp.zeros((block_steps, unit_area), jnp.float32)
    line_duals = jnp.zeros((block_steps, line_limit.shape[0]), jnp.float32)
    totals = []
    for repeat in range(ITERATIONS):
        if repeat == 0:
            injection = demand.astype(jnp.bfloat16)
        else:
            injection = (demand + units_to_bus(power_time, lo_col, hi_row, col_blocks, panel_width)).astype(
                jnp.bfloat16
            )
        sending = jnp.take(injection.reshape(block_steps, col_blocks, panel_width), send_block, axis=1)
        arrived = lax.all_to_all(
            sending.reshape(block_steps, area_devices, capacity, panel_width),
            AREA,
            split_axis=1,
            concat_axis=1,
            tiled=True,
        )
        panels = jnp.take(
            arrived.reshape(block_steps, area_devices * capacity, panel_width), slot_of_tile, axis=1
        )
        partial_value = jnp.einsum(
            "tjb,jlb->tjl", panels, ptdf_tiles, preferred_element_type=jnp.float32
        )
        line_flows = jnp.einsum(
            "tjl,jr->trl", partial_value, row_table, precision=lax.Precision.HIGHEST,
            preferred_element_type=jnp.float32,
        )
        line_flows = line_flows.reshape(block_steps, row_blocks * line_block)
        limits = line_limit[None, :]
        clipped = jnp.clip(line_flows + line_duals, -limits, limits)
        line_duals = line_duals + line_flows - clipped
        excess = line_flows - clipped
        local_total = jnp.sum(excess * excess)
        totals.append(local_total)
        weights = (line_duals + line_flows - clipped).astype(jnp.bfloat16)
        picked = jnp.take(weights.reshape(block_steps, row_blocks, line_block), my_rows, axis=1)
        contrib = jnp.einsum("tjl,jlb->tjb", picked, ptdf_tiles, preferred_element_type=jnp.float32)
        outbound = jnp.einsum(
            "tjb,js->tsb", contrib, slot_table, precision=lax.Precision.HIGHEST,
            preferred_element_type=jnp.float32,
        )
        outbound = outbound.reshape(block_steps, area_devices, capacity, panel_width)
        last = repeat == ITERATIONS - 1
        if last:
            extra = (
                jnp.zeros((block_steps, area_devices, 1, panel_width), jnp.float32)
                .at[0, :, 0, :ITERATIONS]
                .set(jnp.broadcast_to(jnp.stack(totals), (area_devices, ITERATIONS)))
            )
            outbound = jnp.concatenate([outbound, extra], axis=2)
        returned = lax.all_to_all(outbound, AREA, split_axis=1, concat_axis=1, tiled=True)
        if last:
            area_totals = jnp.sum(returned[0, :, capacity, :ITERATIONS], axis=0)
            returned = returned[:, :, :capacity]
        prices = jnp.einsum(
            "tsb,sc->tcb",
            returned.reshape(block_steps, area_devices * capacity, panel_width),
            block_table,
            precision=lax.Precision.HIGHEST,
            preferred_element_type=jnp.float32,
        )
        prices = prices.reshape(block_steps, bus_area)
        gradient = unit_cost + rho_weight * bus_to_units(prices, lo_row, hi_row)
        target = power_time - step_size * gradient
        columns = lax.all_to_all(target, TM, split_axis=1, concat_axis=0, tiled=True)
        spectrum = jnp.dot(
            forward, columns, precision=lax.Precision.HIGHEST, preferred_element_type=jnp.float32
        )
        spectrum_real = spectrum[: half_steps + 1]
        spectrum_imag = jnp.concatenate([empty_row, spectrum[half_steps + 1 :], empty_row], axis=0)
        product_real = spectrum_real * kernel_real - spectrum_imag * kernel_imag
        product_imag = spectrum_real * kernel_imag + spectrum_imag * kernel_real
        stacked = jnp.concatenate([product_real, product_imag[1:half_steps]], axis=0) * row_weight
        smoothed = lax.dot_general(
            forward,
            stacked,
            (((0,), (0,)), ((), ())),
            precision=lax.Precision.HIGHEST,
            preferred_element_type=jnp.float32,
        )
        power_cols = jnp.clip(smoothed, -my_cap[None, :], my_cap[None, :])
        if last:
            chunks = power_cols.reshape(time_devices, block_steps, unit_width)
            extra = (
                jnp.zeros((time_devices, 1, unit_width), jnp.float32)
                .at[:, 0, :ITERATIONS]
                .set(jnp.broadcast_to(area_totals, (time_devices, ITERATIONS)))
            )
            received = lax.all_to_all(
                jnp.concatenate([chunks, extra], axis=1), TM, split_axis=0, concat_axis=0, tiled=True
            )
            summed = jnp.sum(received[:, block_steps, :ITERATIONS], axis=0)
            power_time = jnp.transpose(received[:, :block_steps], (1, 0, 2)).reshape(block_steps, unit_area)
        else:
            power_time = lax.all_to_all(power_cols, TM, split_axis=0, concat_axis=1, tiled=True)
    entries = float(horizon * line_limit.shape[0] * area_devices)
    primal_rms = jnp.sqrt(summed / entries)
    return (power_time, line_duals, primal_rms)


def solution(mesh):
    finer = Mesh(mesh.devices.reshape(16, 4, 4, 2), ("tm_0", "tm_1", "area_0", "area_1"))
    placed = (
        P(TM, AREA),
        P(TM, AREA),
        P(AREA, None, None),
        P(),
        P(),
        P(),
        P(AREA),
        P(AREA),
        P(AREA),
        P(AREA),
        P(),
    )
    return jax.shard_map(
        per_device,
        mesh=finer,
        in_specs=placed,
        out_specs=(P(TM, AREA), P(TM, AREA), P()),
        check_vma=False,
    )
```

```python
import functools
import math

import jax
import jax.numpy as jnp
from jax import lax
from jax.sharding import Mesh
from jax.sharding import PartitionSpec as P
from jax.experimental import pallas as pl

ITERATIONS = 2
TM = ("tm_0", "tm_1")
AREA = ("area_0", "area_1")
TM_AREA = ("tm_0", "tm_1", "area_0", "area_1")


step_size = 0.5
rho_weight = 1.0


def laid_out(tiles, dim):
    dims = list(tiles.shape[1:])
    dims[dim] *= tiles.shape[0]
    return jnp.moveaxis(tiles, 0, dim).reshape(dims)


def copy_for_each(array, axis):
    count = lax.axis_size(axis)
    return lax.all_to_all(
        jnp.broadcast_to(array[None], (count, *array.shape)), axis, 0, 0, tiled=True
    )


def collect(array, axis, dim):
    return laid_out(copy_for_each(array, axis), dim)


PARTS = 2
ROWS = 16
UNIT_BLOCK = 1024


def split_parts(values):
    pieces = []
    rest = values
    for _ in range(PARTS):
        piece = rest.astype(jnp.bfloat16)
        pieces.append(piece)
        rest = rest - piece.astype(jnp.float32)
    return pieces


def group_targets(group):
    half = (lax.broadcasted_iota(jnp.int32, (ROWS, 1), 0) >= ROWS // 2).astype(jnp.int32)
    return 2 * group + half


def gather_kernel(table_ref, lo_ref, hi_ref, out_ref):
    lanes = table_ref.shape[1]
    width = lo_ref.shape[1]
    onehot = (lax.broadcasted_iota(jnp.int32, (lanes, width), 0) == lo_ref[...]).astype(jnp.bfloat16)
    picked = jnp.dot(table_ref[...], onehot, preferred_element_type=jnp.float32)
    hi = hi_ref[...]
    total = jnp.zeros((ROWS, width), jnp.float32)
    for group in range(table_ref.shape[0] // ROWS):
        block = picked[group * ROWS : (group + 1) * ROWS]
        total = total + jnp.where(hi == group_targets(group), block, 0.0)
    out_ref[...] = total


def bus_to_units(prices, lo_row, hi_row):
    steps, buses = prices.shape
    panel = 256
    blocks = buses // panel
    groups = (blocks + 1) // 2
    units = lo_row.shape[1]
    pieces = jnp.stack(split_parts(prices.reshape(steps, blocks, panel)), axis=0)
    pieces = jnp.pad(pieces, ((0, 0), (0, 0), (0, 2 * groups - blocks), (0, 0)))
    pieces = pieces.reshape(PARTS, steps, groups, 2, panel)
    table = jnp.transpose(pieces, (2, 3, 0, 1, 4)).reshape(groups * ROWS, panel)
    picked = pl.pallas_call(
        gather_kernel,
        grid=(units // UNIT_BLOCK,),
        in_specs=[
            pl.BlockSpec((groups * ROWS, panel), lambda i: (0, 0)),
            pl.BlockSpec((1, UNIT_BLOCK), lambda i: (0, i)),
            pl.BlockSpec((1, UNIT_BLOCK), lambda i: (0, i)),
        ],
        out_specs=pl.BlockSpec((ROWS, UNIT_BLOCK), lambda i: (0, i)),
        out_shape=jax.ShapeDtypeStruct((ROWS, units), jnp.float32),
    )(table, lo_row, hi_row)
    return jnp.sum(picked.reshape(ROWS // steps, steps, units), axis=0)


def scatter_kernel(parts_ref, lo_ref, hi_ref, out_ref):
    @pl.when(pl.program_id(0) == 0)
    def _():
        out_ref[...] = jnp.zeros(out_ref.shape, out_ref.dtype)

    width = parts_ref.shape[1]
    lanes = out_ref.shape[1]
    onehot = (lax.broadcasted_iota(jnp.int32, (width, lanes), 1) == lo_ref[...]).astype(jnp.bfloat16)
    parts = parts_ref[...]
    hi = hi_ref[...]
    masked = jnp.concatenate(
        [
            jnp.where(hi == group_targets(group), parts, jnp.zeros_like(parts))
            for group in range(out_ref.shape[0] // ROWS)
        ],
        axis=0,
    )
    out_ref[...] += jnp.dot(masked, onehot, preferred_element_type=jnp.float32)


def units_to_bus(power, lo_col, hi_row, blocks, panel):
    steps, units = power.shape
    groups = (blocks + 1) // 2
    pieces = split_parts(power)
    parts = jnp.concatenate(pieces + pieces, axis=0)
    summed = pl.pallas_call(
        scatter_kernel,
        grid=(units // UNIT_BLOCK,),
        in_specs=[
            pl.BlockSpec((ROWS, UNIT_BLOCK), lambda i: (0, i)),
            pl.BlockSpec((UNIT_BLOCK, 1), lambda i: (i, 0)),
            pl.BlockSpec((1, UNIT_BLOCK), lambda i: (0, i)),
        ],
        out_specs=pl.BlockSpec((groups * ROWS, panel), lambda i: (0, 0)),
        out_shape=jax.ShapeDtypeStruct((groups * ROWS, panel), jnp.float32),
    )(parts, lo_col, hi_row)
    summed = jnp.sum(summed.reshape(groups, 2, PARTS, steps, panel), axis=2)
    summed = jnp.transpose(summed, (2, 0, 1, 3)).reshape(steps, 2 * groups * panel)
    return summed[:, : blocks * panel]


def one_axis_at_a_time(array, axes):
    return functools.reduce(lax.psum, axes, array)


def per_device(
    demand,
    unit_cost,
    ptdf_tiles,
    tile_area,
    tile_block,
    tile_row,
    unit_bus,
    unit_class,
    power_cap,
    line_limit,
    smoother,
):
    time_devices = lax.axis_size(TM)
    area_devices = lax.axis_size(AREA)
    block_steps, bus_area = demand.shape
    unit_area = unit_cost.shape[1]
    tile_count, line_block, panel_width = ptdf_tiles.shape
    col_blocks = bus_area // panel_width
    row_blocks = line_limit.shape[0] // line_block
    capacity = 2 * tile_count // area_devices
    horizon = block_steps * time_devices
    unit_width = unit_area // time_devices
    area_index = lax.axis_index(AREA)
    time_index = lax.axis_index(TM)
    tile_areas = tile_area.reshape(area_devices, tile_count)
    block_grid = tile_block.reshape(area_devices, tile_count)
    row_grid = tile_row.reshape(area_devices, tile_count)
    is_source = (tile_areas == area_index).astype(jnp.int32)
    rank_source = jnp.cumsum(is_source, axis=1) - 1
    slot_ids = jnp.arange(capacity, dtype=jnp.int32)
    chosen = is_source[:, None, :] * (rank_source[:, None, :] == slot_ids[None, :, None]).astype(
        jnp.int32
    )
    send_block = jnp.sum(chosen * block_grid[:, None, :], axis=2).reshape(-1)
    my_areas = lax.dynamic_index_in_dim(tile_areas, area_index, 0, keepdims=False)
    my_blocks = lax.dynamic_index_in_dim(block_grid, area_index, 0, keepdims=False)
    my_rows = lax.dynamic_index_in_dim(row_grid, area_index, 0, keepdims=False)
    positions = jnp.arange(tile_count, dtype=jnp.int32)
    earlier = positions[None, :] <= positions[:, None]
    same_area = my_areas[None, :] == my_areas[:, None]
    rank_mine = jnp.sum((same_area & earlier).astype(jnp.int32), axis=1) - 1
    slot_of_tile = my_areas * capacity + rank_mine
    my_columns = my_areas * col_blocks + my_blocks
    my_class = lax.dynamic_slice_in_dim(unit_class, time_index * unit_width, unit_width)
    my_cap = lax.dynamic_slice_in_dim(power_cap, time_index * unit_width, unit_width)
    half_steps = horizon // 2
    steps_line = jnp.arange(horizon, dtype=jnp.int32)
    frequency = jnp.concatenate(
        [jnp.arange(half_steps + 1, dtype=jnp.int32), jnp.arange(1, half_steps, dtype=jnp.int32)]
    )
    angle = (frequency[:, None] * steps_line[None, :] % horizon).astype(jnp.float32) * (
        2.0 * math.pi / horizon
    )
    cosine_rows = (steps_line <= half_steps)[:, None]
    forward = jnp.where(cosine_rows, jnp.cos(angle), -jnp.sin(angle))
    edge_rows = (frequency == 0) | (frequency == half_steps)
    row_weight = (jnp.where(edge_rows, 1.0, 2.0).astype(jnp.float32) / horizon)[:, None]
    kernel_spectrum = jnp.dot(
        forward, smoother.T, precision=lax.Precision.HIGHEST, preferred_element_type=jnp.float32
    )
    class_table = (
        my_class[None, :] == jnp.arange(smoother.shape[0], dtype=jnp.int32)[:, None]
    ).astype(jnp.float32)
    unit_spectrum = jnp.dot(
        kernel_spectrum,
        class_table,
        precision=lax.Precision.HIGHEST,
        preferred_element_type=jnp.float32,
    )
    empty_row = jnp.zeros((1, unit_width), jnp.float32)
    kernel_real = unit_spectrum[: half_steps + 1]
    kernel_imag = jnp.concatenate([empty_row, unit_spectrum[half_steps + 1 :], empty_row], axis=0)
    row_table = (my_rows[:, None] == jnp.arange(row_blocks, dtype=jnp.int32)[None, :]).astype(jnp.float32)
    slot_table = (
        slot_of_tile[:, None] == jnp.arange(area_devices * capacity, dtype=jnp.int32)[None, :]
    ).astype(jnp.float32)
    block_table = (send_block[:, None] == jnp.arange(col_blocks, dtype=jnp.int32)[None, :]).astype(jnp.float32)
    lo_row = (unit_bus % panel_width).reshape(1, unit_area)
    hi_row = (unit_bus // panel_width).reshape(1, unit_area)
    lo_col = lo_row.reshape(unit_area, 1)
    power_time = jnp.zeros((block_steps, unit_area), jnp.float32)
    line_duals = jnp.zeros((block_steps, line_limit.shape[0]), jnp.float32)
    totals = []
    for repeat in range(ITERATIONS):
        if repeat == 0:
            injection = demand.astype(jnp.bfloat16)
        else:
            injection = (demand + units_to_bus(power_time, lo_col, hi_row, col_blocks, panel_width)).astype(
                jnp.bfloat16
            )
        sending = jnp.take(injection.reshape(block_steps, col_blocks, panel_width), send_block, axis=1)
        arrived = lax.all_to_all(
            sending.reshape(block_steps, area_devices, capacity, panel_width),
            AREA,
            split_axis=1,
            concat_axis=1,
            tiled=True,
        )
        panels = jnp.take(
            arrived.reshape(block_steps, area_devices * capacity, panel_width), slot_of_tile, axis=1
        )
        partial_value = jnp.einsum(
            "tjb,jlb->tjl", panels, ptdf_tiles, preferred_element_type=jnp.float32
        )
        line_flows = jnp.einsum(
            "tjl,jr->trl", partial_value, row_table, precision=lax.Precision.HIGHEST,
            preferred_element_type=jnp.float32,
        )
        line_flows = line_flows.reshape(block_steps, row_blocks * line_block)
        limits = line_limit[None, :]
        clipped = jnp.clip(line_flows + line_duals, -limits, limits)
        line_duals = line_duals + line_flows - clipped
        excess = line_flows - clipped
        local_total = jnp.sum(excess * excess)
        totals.append(local_total)
        weights = (line_duals + line_flows - clipped).astype(jnp.bfloat16)
        picked = jnp.take(weights.reshape(block_steps, row_blocks, line_block), my_rows, axis=1)
        contrib = jnp.einsum("tjl,jlb->tjb", picked, ptdf_tiles, preferred_element_type=jnp.float32)
        outbound = jnp.einsum(
            "tjb,js->tsb", contrib, slot_table, precision=lax.Precision.HIGHEST,
            preferred_element_type=jnp.float32,
        )
        outbound = outbound.reshape(block_steps, area_devices, capacity, panel_width)
        last = repeat == ITERATIONS - 1
        if last:
            extra = (
                jnp.zeros((block_steps, area_devices, 1, panel_width), jnp.float32)
                .at[0, :, 0, :ITERATIONS]
                .set(jnp.broadcast_to(jnp.stack(totals), (area_devices, ITERATIONS)))
            )
            outbound = jnp.concatenate([outbound, extra], axis=2)
        returned = lax.all_to_all(outbound, AREA, split_axis=1, concat_axis=1, tiled=True)
        if last:
            area_totals = jnp.sum(returned[0, :, capacity, :ITERATIONS], axis=0)
            returned = returned[:, :, :capacity]
        prices = jnp.einsum(
            "tsb,sc->tcb",
            returned.reshape(block_steps, area_devices * capacity, panel_width),
            block_table,
            precision=lax.Precision.HIGHEST,
            preferred_element_type=jnp.float32,
        )
        prices = prices.reshape(block_steps, bus_area)
        gradient = unit_cost + rho_weight * bus_to_units(prices, lo_row, hi_row)
        target = power_time - step_size * gradient
        columns = lax.all_to_all(target, TM, split_axis=1, concat_axis=0, tiled=True)
        spectrum = jnp.dot(
            forward, columns, precision=lax.Precision.HIGHEST, preferred_element_type=jnp.float32
        )
        spectrum_real = spectrum[: half_steps + 1]
        spectrum_imag = jnp.concatenate([empty_row, spectrum[half_steps + 1 :], empty_row], axis=0)
        product_real = spectrum_real * kernel_real - spectrum_imag * kernel_imag
        product_imag = spectrum_real * kernel_imag + spectrum_imag * kernel_real
        stacked = jnp.concatenate([product_real, product_imag[1:half_steps]], axis=0) * row_weight
        smoothed = lax.dot_general(
            forward,
            stacked,
            (((0,), (0,)), ((), ())),
            precision=lax.Precision.HIGHEST,
            preferred_element_type=jnp.float32,
        )
        power_cols = jnp.clip(smoothed, -my_cap[None, :], my_cap[None, :])
        if last:
            chunks = power_cols.reshape(time_devices, block_steps, unit_width)
            extra = (
                jnp.zeros((time_devices, 1, unit_width), jnp.float32)
                .at[:, 0, :ITERATIONS]
                .set(jnp.broadcast_to(area_totals, (time_devices, ITERATIONS)))
            )
            received = lax.all_to_all(
                jnp.concatenate([chunks, extra], axis=1), TM, split_axis=0, concat_axis=0, tiled=True
            )
            summed = jnp.sum(received[:, block_steps, :ITERATIONS], axis=0)
            power_time = jnp.transpose(received[:, :block_steps], (1, 0, 2)).reshape(block_steps, unit_area)
        else:
            power_time = lax.all_to_all(power_cols, TM, split_axis=0, concat_axis=1, tiled=True)
    entries = float(horizon * line_limit.shape[0] * area_devices)
    primal_rms = jnp.sqrt(summed / entries)
    return (power_time, line_duals, primal_rms)


def solution(mesh):
    finer = Mesh(mesh.devices.reshape(16, 4, 4, 2), ("tm_0", "tm_1", "area_0", "area_1"))
    placed = (
        P(TM, AREA),
        P(TM, AREA),
        P(AREA, None, None),
        P(),
        P(),
        P(),
        P(AREA),
        P(AREA),
        P(AREA),
        P(AREA),
        P(),
    )
    return jax.shard_map(
        per_device,
        mesh=finer,
        in_specs=placed,
        out_specs=(P(TM, AREA), P(TM, AREA), P()),
        check_vma=False,
    )
```

```python
import functools
import math

import jax
import jax.numpy as jnp
from jax import lax
from jax.sharding import Mesh
from jax.sharding import PartitionSpec as P
from jax.experimental import pallas as pl

ITERATIONS = 2
TM = ("tm_0", "tm_1")
AREA = ("area_0", "area_1")
TM_AREA = ("tm_0", "tm_1", "area_0", "area_1")


step_size = 0.5
rho_weight = 1.0


def laid_out(tiles, dim):
    dims = list(tiles.shape[1:])
    dims[dim] *= tiles.shape[0]
    return jnp.moveaxis(tiles, 0, dim).reshape(dims)


def copy_for_each(array, axis):
    count = lax.axis_size(axis)
    return lax.all_to_all(
        jnp.broadcast_to(array[None], (count, *array.shape)), axis, 0, 0, tiled=True
    )


def collect(array, axis, dim):
    return laid_out(copy_for_each(array, axis), dim)


PARTS = 2
ROWS = 16
UNIT_BLOCK = 2048


def split_parts(values):
    pieces = []
    rest = values
    for _ in range(PARTS):
        piece = rest.astype(jnp.bfloat16)
        pieces.append(piece)
        rest = rest - piece.astype(jnp.float32)
    return pieces


def group_targets(group):
    half = (lax.broadcasted_iota(jnp.int32, (ROWS, 1), 0) >= ROWS // 2).astype(jnp.int32)
    return 2 * group + half


def gather_kernel(table_ref, lo_ref, hi_ref, out_ref):
    lanes = table_ref.shape[1]
    width = lo_ref.shape[1]
    onehot = (lax.broadcasted_iota(jnp.int32, (lanes, width), 0) == lo_ref[...]).astype(jnp.bfloat16)
    picked = jnp.dot(table_ref[...], onehot, preferred_element_type=jnp.float32)
    hi = hi_ref[...]
    total = jnp.zeros((ROWS, width), jnp.float32)
    for group in range(table_ref.shape[0] // ROWS):
        block = picked[group * ROWS : (group + 1) * ROWS]
        total = total + jnp.where(hi == group_targets(group), block, 0.0)
    out_ref[...] = total


def bus_to_units(prices, lo_row, hi_row):
    steps, buses = prices.shape
    panel = 256
    blocks = buses // panel
    groups = (blocks + 1) // 2
    units = lo_row.shape[1]
    pieces = jnp.stack(split_parts(prices.reshape(steps, blocks, panel)), axis=0)
    pieces = jnp.pad(pieces, ((0, 0), (0, 0), (0, 2 * groups - blocks), (0, 0)))
    pieces = pieces.reshape(PARTS, steps, groups, 2, panel)
    table = jnp.transpose(pieces, (2, 3, 0, 1, 4)).reshape(groups * ROWS, panel)
    picked = pl.pallas_call(
        gather_kernel,
        grid=(units // UNIT_BLOCK,),
        in_specs=[
            pl.BlockSpec((groups * ROWS, panel), lambda i: (0, 0)),
            pl.BlockSpec((1, UNIT_BLOCK), lambda i: (0, i)),
            pl.BlockSpec((1, UNIT_BLOCK), lambda i: (0, i)),
        ],
        out_specs=pl.BlockSpec((ROWS, UNIT_BLOCK), lambda i: (0, i)),
        out_shape=jax.ShapeDtypeStruct((ROWS, units), jnp.float32),
    )(table, lo_row, hi_row)
    return jnp.sum(picked.reshape(ROWS // steps, steps, units), axis=0)


def scatter_kernel(parts_ref, lo_ref, hi_ref, out_ref):
    @pl.when(pl.program_id(0) == 0)
    def _():
        out_ref[...] = jnp.zeros(out_ref.shape, out_ref.dtype)

    width = parts_ref.shape[1]
    lanes = out_ref.shape[1]
    onehot = (lax.broadcasted_iota(jnp.int32, (width, lanes), 1) == lo_ref[...]).astype(jnp.bfloat16)
    parts = parts_ref[...]
    hi = hi_ref[...]
    masked = jnp.concatenate(
        [
            jnp.where(hi == group_targets(group), parts, jnp.zeros_like(parts))
            for group in range(out_ref.shape[0] // ROWS)
        ],
        axis=0,
    )
    out_ref[...] += jnp.dot(masked, onehot, preferred_element_type=jnp.float32)


def units_to_bus(power, lo_col, hi_row, blocks, panel):
    steps, units = power.shape
    groups = (blocks + 1) // 2
    pieces = split_parts(power)
    parts = jnp.concatenate(pieces + pieces, axis=0)
    summed = pl.pallas_call(
        scatter_kernel,
        grid=(units // UNIT_BLOCK,),
        in_specs=[
            pl.BlockSpec((ROWS, UNIT_BLOCK), lambda i: (0, i)),
            pl.BlockSpec((UNIT_BLOCK, 1), lambda i: (i, 0)),
            pl.BlockSpec((1, UNIT_BLOCK), lambda i: (0, i)),
        ],
        out_specs=pl.BlockSpec((groups * ROWS, panel), lambda i: (0, 0)),
        out_shape=jax.ShapeDtypeStruct((groups * ROWS, panel), jnp.float32),
    )(parts, lo_col, hi_row)
    summed = jnp.sum(summed.reshape(groups, 2, PARTS, steps, panel), axis=2)
    summed = jnp.transpose(summed, (2, 0, 1, 3)).reshape(steps, 2 * groups * panel)
    return summed[:, : blocks * panel]


def one_axis_at_a_time(array, axes):
    return functools.reduce(lax.psum, axes, array)


def per_device(
    demand,
    unit_cost,
    ptdf_tiles,
    tile_area,
    tile_block,
    tile_row,
    unit_bus,
    unit_class,
    power_cap,
    line_limit,
    smoother,
):
    time_devices = lax.axis_size(TM)
    area_devices = lax.axis_size(AREA)
    block_steps, bus_area = demand.shape
    unit_area = unit_cost.shape[1]
    tile_count, line_block, panel_width = ptdf_tiles.shape
    col_blocks = bus_area // panel_width
    row_blocks = line_limit.shape[0] // line_block
    capacity = 2 * tile_count // area_devices
    horizon = block_steps * time_devices
    unit_width = unit_area // time_devices
    area_index = lax.axis_index(AREA)
    time_index = lax.axis_index(TM)
    tile_areas = tile_area.reshape(area_devices, tile_count)
    block_grid = tile_block.reshape(area_devices, tile_count)
    row_grid = tile_row.reshape(area_devices, tile_count)
    is_source = (tile_areas == area_index).astype(jnp.int32)
    rank_source = jnp.cumsum(is_source, axis=1) - 1
    slot_ids = jnp.arange(capacity, dtype=jnp.int32)
    chosen = is_source[:, None, :] * (rank_source[:, None, :] == slot_ids[None, :, None]).astype(
        jnp.int32
    )
    send_block = jnp.sum(chosen * block_grid[:, None, :], axis=2).reshape(-1)
    my_areas = lax.dynamic_index_in_dim(tile_areas, area_index, 0, keepdims=False)
    my_blocks = lax.dynamic_index_in_dim(block_grid, area_index, 0, keepdims=False)
    my_rows = lax.dynamic_index_in_dim(row_grid, area_index, 0, keepdims=False)
    positions = jnp.arange(tile_count, dtype=jnp.int32)
    earlier = positions[None, :] <= positions[:, None]
    same_area = my_areas[None, :] == my_areas[:, None]
    rank_mine = jnp.sum((same_area & earlier).astype(jnp.int32), axis=1) - 1
    slot_of_tile = my_areas * capacity + rank_mine
    my_columns = my_areas * col_blocks + my_blocks
    my_class = lax.dynamic_slice_in_dim(unit_class, time_index * unit_width, unit_width)
    my_cap = lax.dynamic_slice_in_dim(power_cap, time_index * unit_width, unit_width)
    half_steps = horizon // 2
    steps_line = jnp.arange(horizon, dtype=jnp.int32)
    frequency = jnp.concatenate(
        [jnp.arange(half_steps + 1, dtype=jnp.int32), jnp.arange(1, half_steps, dtype=jnp.int32)]
    )
    angle = (frequency[:, None] * steps_line[None, :] % horizon).astype(jnp.float32) * (
        2.0 * math.pi / horizon
    )
    cosine_rows = (steps_line <= half_steps)[:, None]
    forward = jnp.where(cosine_rows, jnp.cos(angle), -jnp.sin(angle))
    edge_rows = (frequency == 0) | (frequency == half_steps)
    row_weight = (jnp.where(edge_rows, 1.0, 2.0).astype(jnp.float32) / horizon)[:, None]
    kernel_spectrum = jnp.dot(
        forward, smoother.T, precision=lax.Precision.HIGHEST, preferred_element_type=jnp.float32
    )
    class_table = (
        my_class[None, :] == jnp.arange(smoother.shape[0], dtype=jnp.int32)[:, None]
    ).astype(jnp.float32)
    unit_spectrum = jnp.dot(
        kernel_spectrum,
        class_table,
        precision=lax.Precision.HIGHEST,
        preferred_element_type=jnp.float32,
    )
    empty_row = jnp.zeros((1, unit_width), jnp.float32)
    kernel_real = unit_spectrum[: half_steps + 1]
    kernel_imag = jnp.concatenate([empty_row, unit_spectrum[half_steps + 1 :], empty_row], axis=0)
    row_table = (my_rows[:, None] == jnp.arange(row_blocks, dtype=jnp.int32)[None, :]).astype(jnp.float32)
    slot_table = (
        slot_of_tile[:, None] == jnp.arange(area_devices * capacity, dtype=jnp.int32)[None, :]
    ).astype(jnp.float32)
    block_table = (send_block[:, None] == jnp.arange(col_blocks, dtype=jnp.int32)[None, :]).astype(jnp.float32)
    lo_row = (unit_bus % panel_width).reshape(1, unit_area)
    hi_row = (unit_bus // panel_width).reshape(1, unit_area)
    lo_col = lo_row.reshape(unit_area, 1)
    power_time = jnp.zeros((block_steps, unit_area), jnp.float32)
    line_duals = jnp.zeros((block_steps, line_limit.shape[0]), jnp.float32)
    totals = []
    for repeat in range(ITERATIONS):
        if repeat == 0:
            injection = demand.astype(jnp.bfloat16)
        else:
            injection = (demand + units_to_bus(power_time, lo_col, hi_row, col_blocks, panel_width)).astype(
                jnp.bfloat16
            )
        sending = jnp.take(injection.reshape(block_steps, col_blocks, panel_width), send_block, axis=1)
        arrived = lax.all_to_all(
            sending.reshape(block_steps, area_devices, capacity, panel_width),
            AREA,
            split_axis=1,
            concat_axis=1,
            tiled=True,
        )
        panels = jnp.take(
            arrived.reshape(block_steps, area_devices * capacity, panel_width), slot_of_tile, axis=1
        )
        partial_value = jnp.einsum(
            "tjb,jlb->tjl", panels, ptdf_tiles, preferred_element_type=jnp.float32
        )
        line_flows = jnp.einsum(
            "tjl,jr->trl", partial_value, row_table, precision=lax.Precision.HIGHEST,
            preferred_element_type=jnp.float32,
        )
        line_flows = line_flows.reshape(block_steps, row_blocks * line_block)
        limits = line_limit[None, :]
        clipped = jnp.clip(line_flows + line_duals, -limits, limits)
        line_duals = line_duals + line_flows - clipped
        excess = line_flows - clipped
        local_total = jnp.sum(excess * excess)
        totals.append(local_total)
        weights = (line_duals + line_flows - clipped).astype(jnp.bfloat16)
        picked = jnp.take(weights.reshape(block_steps, row_blocks, line_block), my_rows, axis=1)
        contrib = jnp.einsum("tjl,jlb->tjb", picked, ptdf_tiles, preferred_element_type=jnp.float32)
        outbound = jnp.einsum(
            "tjb,js->tsb", contrib, slot_table, precision=lax.Precision.HIGHEST,
            preferred_element_type=jnp.float32,
        )
        outbound = outbound.reshape(block_steps, area_devices, capacity, panel_width)
        last = repeat == ITERATIONS - 1
        if last:
            extra = (
                jnp.zeros((block_steps, area_devices, 1, panel_width), jnp.float32)
                .at[0, :, 0, :ITERATIONS]
                .set(jnp.broadcast_to(jnp.stack(totals), (area_devices, ITERATIONS)))
            )
            outbound = jnp.concatenate([outbound, extra], axis=2)
        returned = lax.all_to_all(outbound, AREA, split_axis=1, concat_axis=1, tiled=True)
        if last:
            area_totals = jnp.sum(returned[0, :, capacity, :ITERATIONS], axis=0)
            returned = returned[:, :, :capacity]
        prices = jnp.einsum(
            "tsb,sc->tcb",
            returned.reshape(block_steps, area_devices * capacity, panel_width),
            block_table,
            precision=lax.Precision.HIGHEST,
            preferred_element_type=jnp.float32,
        )
        prices = prices.reshape(block_steps, bus_area)
        gradient = unit_cost + rho_weight * bus_to_units(prices, lo_row, hi_row)
        target = power_time - step_size * gradient
        columns = lax.all_to_all(target, TM, split_axis=1, concat_axis=0, tiled=True)
        spectrum = jnp.dot(
            forward, columns, precision=lax.Precision.HIGHEST, preferred_element_type=jnp.float32
        )
        spectrum_real = spectrum[: half_steps + 1]
        spectrum_imag = jnp.concatenate([empty_row, spectrum[half_steps + 1 :], empty_row], axis=0)
        product_real = spectrum_real * kernel_real - spectrum_imag * kernel_imag
        product_imag = spectrum_real * kernel_imag + spectrum_imag * kernel_real
        stacked = jnp.concatenate([product_real, product_imag[1:half_steps]], axis=0) * row_weight
        smoothed = lax.dot_general(
            forward,
            stacked,
            (((0,), (0,)), ((), ())),
            precision=lax.Precision.HIGHEST,
            preferred_element_type=jnp.float32,
        )
        power_cols = jnp.clip(smoothed, -my_cap[None, :], my_cap[None, :])
        if last:
            chunks = power_cols.reshape(time_devices, block_steps, unit_width)
            extra = (
                jnp.zeros((time_devices, 1, unit_width), jnp.float32)
                .at[:, 0, :ITERATIONS]
                .set(jnp.broadcast_to(area_totals, (time_devices, ITERATIONS)))
            )
            received = lax.all_to_all(
                jnp.concatenate([chunks, extra], axis=1), TM, split_axis=0, concat_axis=0, tiled=True
            )
            summed = jnp.sum(received[:, block_steps, :ITERATIONS], axis=0)
            power_time = jnp.transpose(received[:, :block_steps], (1, 0, 2)).reshape(block_steps, unit_area)
        else:
            power_time = lax.all_to_all(power_cols, TM, split_axis=0, concat_axis=1, tiled=True)
    entries = float(horizon * line_limit.shape[0] * area_devices)
    primal_rms = jnp.sqrt(summed / entries)
    return (power_time, line_duals, primal_rms)


def solution(mesh):
    finer = Mesh(mesh.devices.reshape(16, 4, 4, 2), ("tm_0", "tm_1", "area_0", "area_1"))
    placed = (
        P(TM, AREA),
        P(TM, AREA),
        P(AREA, None, None),
        P(),
        P(),
        P(),
        P(AREA),
        P(AREA),
        P(AREA),
        P(AREA),
        P(),
    )
    return jax.shard_map(
        per_device,
        mesh=finer,
        in_specs=placed,
        out_specs=(P(TM, AREA), P(TM, AREA), P()),
        check_vma=False,
    )
```

```python
import functools
import math

import jax
import jax.numpy as jnp
from jax import lax
from jax.sharding import Mesh
from jax.sharding import PartitionSpec as P
from jax.experimental import pallas as pl

ITERATIONS = 2
TM = ("tm_0", "tm_1")
AREA = ("area_0", "area_1")
TM_AREA = ("tm_0", "tm_1", "area_0", "area_1")


step_size = 0.5
rho_weight = 1.0


def laid_out(tiles, dim):
    dims = list(tiles.shape[1:])
    dims[dim] *= tiles.shape[0]
    return jnp.moveaxis(tiles, 0, dim).reshape(dims)


def copy_for_each(array, axis):
    count = lax.axis_size(axis)
    return lax.all_to_all(
        jnp.broadcast_to(array[None], (count, *array.shape)), axis, 0, 0, tiled=True
    )


def collect(array, axis, dim):
    return laid_out(copy_for_each(array, axis), dim)


PARTS = 2
ROWS = 16
UNIT_BLOCK = 4096


def split_parts(values):
    pieces = []
    rest = values
    for _ in range(PARTS):
        piece = rest.astype(jnp.bfloat16)
        pieces.append(piece)
        rest = rest - piece.astype(jnp.float32)
    return pieces


def group_targets(group):
    half = (lax.broadcasted_iota(jnp.int32, (ROWS, 1), 0) >= ROWS // 2).astype(jnp.int32)
    return 2 * group + half


def gather_kernel(table_ref, lo_ref, hi_ref, out_ref):
    lanes = table_ref.shape[1]
    width = lo_ref.shape[1]
    onehot = (lax.broadcasted_iota(jnp.int32, (lanes, width), 0) == lo_ref[...]).astype(jnp.bfloat16)
    picked = jnp.dot(table_ref[...], onehot, preferred_element_type=jnp.float32)
    hi = hi_ref[...]
    total = jnp.zeros((ROWS, width), jnp.float32)
    for group in range(table_ref.shape[0] // ROWS):
        block = picked[group * ROWS : (group + 1) * ROWS]
        total = total + jnp.where(hi == group_targets(group), block, 0.0)
    out_ref[...] = total


def bus_to_units(prices, lo_row, hi_row):
    steps, buses = prices.shape
    panel = 256
    blocks = buses // panel
    groups = (blocks + 1) // 2
    units = lo_row.shape[1]
    pieces = jnp.stack(split_parts(prices.reshape(steps, blocks, panel)), axis=0)
    pieces = jnp.pad(pieces, ((0, 0), (0, 0), (0, 2 * groups - blocks), (0, 0)))
    pieces = pieces.reshape(PARTS, steps, groups, 2, panel)
    table = jnp.transpose(pieces, (2, 3, 0, 1, 4)).reshape(groups * ROWS, panel)
    picked = pl.pallas_call(
        gather_kernel,
        grid=(units // UNIT_BLOCK,),
        in_specs=[
            pl.BlockSpec((groups * ROWS, panel), lambda i: (0, 0)),
            pl.BlockSpec((1, UNIT_BLOCK), lambda i: (0, i)),
            pl.BlockSpec((1, UNIT_BLOCK), lambda i: (0, i)),
        ],
        out_specs=pl.BlockSpec((ROWS, UNIT_BLOCK), lambda i: (0, i)),
        out_shape=jax.ShapeDtypeStruct((ROWS, units), jnp.float32),
    )(table, lo_row, hi_row)
    return jnp.sum(picked.reshape(ROWS // steps, steps, units), axis=0)


def scatter_kernel(parts_ref, lo_ref, hi_ref, out_ref):
    @pl.when(pl.program_id(0) == 0)
    def _():
        out_ref[...] = jnp.zeros(out_ref.shape, out_ref.dtype)

    width = parts_ref.shape[1]
    lanes = out_ref.shape[1]
    onehot = (lax.broadcasted_iota(jnp.int32, (width, lanes), 1) == lo_ref[...]).astype(jnp.bfloat16)
    parts = parts_ref[...]
    hi = hi_ref[...]
    masked = jnp.concatenate(
        [
            jnp.where(hi == group_targets(group), parts, jnp.zeros_like(parts))
            for group in range(out_ref.shape[0] // ROWS)
        ],
        axis=0,
    )
    out_ref[...] += jnp.dot(masked, onehot, preferred_element_type=jnp.float32)


def units_to_bus(power, lo_col, hi_row, blocks, panel):
    steps, units = power.shape
    groups = (blocks + 1) // 2
    pieces = split_parts(power)
    parts = jnp.concatenate(pieces + pieces, axis=0)
    summed = pl.pallas_call(
        scatter_kernel,
        grid=(units // UNIT_BLOCK,),
        in_specs=[
            pl.BlockSpec((ROWS, UNIT_BLOCK), lambda i: (0, i)),
            pl.BlockSpec((UNIT_BLOCK, 1), lambda i: (i, 0)),
            pl.BlockSpec((1, UNIT_BLOCK), lambda i: (0, i)),
        ],
        out_specs=pl.BlockSpec((groups * ROWS, panel), lambda i: (0, 0)),
        out_shape=jax.ShapeDtypeStruct((groups * ROWS, panel), jnp.float32),
    )(parts, lo_col, hi_row)
    summed = jnp.sum(summed.reshape(groups, 2, PARTS, steps, panel), axis=2)
    summed = jnp.transpose(summed, (2, 0, 1, 3)).reshape(steps, 2 * groups * panel)
    return summed[:, : blocks * panel]


def one_axis_at_a_time(array, axes):
    return functools.reduce(lax.psum, axes, array)


def per_device(
    demand,
    unit_cost,
    ptdf_tiles,
    tile_area,
    tile_block,
    tile_row,
    unit_bus,
    unit_class,
    power_cap,
    line_limit,
    smoother,
):
    time_devices = lax.axis_size(TM)
    area_devices = lax.axis_size(AREA)
    block_steps, bus_area = demand.shape
    unit_area = unit_cost.shape[1]
    tile_count, line_block, panel_width = ptdf_tiles.shape
    col_blocks = bus_area // panel_width
    row_blocks = line_limit.shape[0] // line_block
    capacity = 2 * tile_count // area_devices
    horizon = block_steps * time_devices
    unit_width = unit_area // time_devices
    area_index = lax.axis_index(AREA)
    time_index = lax.axis_index(TM)
    tile_areas = tile_area.reshape(area_devices, tile_count)
    block_grid = tile_block.reshape(area_devices, tile_count)
    row_grid = tile_row.reshape(area_devices, tile_count)
    is_source = (tile_areas == area_index).astype(jnp.int32)
    rank_source = jnp.cumsum(is_source, axis=1) - 1
    slot_ids = jnp.arange(capacity, dtype=jnp.int32)
    chosen = is_source[:, None, :] * (rank_source[:, None, :] == slot_ids[None, :, None]).astype(
        jnp.int32
    )
    send_block = jnp.sum(chosen * block_grid[:, None, :], axis=2).reshape(-1)
    my_areas = lax.dynamic_index_in_dim(tile_areas, area_index, 0, keepdims=False)
    my_blocks = lax.dynamic_index_in_dim(block_grid, area_index, 0, keepdims=False)
    my_rows = lax.dynamic_index_in_dim(row_grid, area_index, 0, keepdims=False)
    positions = jnp.arange(tile_count, dtype=jnp.int32)
    earlier = positions[None, :] <= positions[:, None]
    same_area = my_areas[None, :] == my_areas[:, None]
    rank_mine = jnp.sum((same_area & earlier).astype(jnp.int32), axis=1) - 1
    slot_of_tile = my_areas * capacity + rank_mine
    my_columns = my_areas * col_blocks + my_blocks
    my_class = lax.dynamic_slice_in_dim(unit_class, time_index * unit_width, unit_width)
    my_cap = lax.dynamic_slice_in_dim(power_cap, time_index * unit_width, unit_width)
    half_steps = horizon // 2
    steps_line = jnp.arange(horizon, dtype=jnp.int32)
    frequency = jnp.concatenate(
        [jnp.arange(half_steps + 1, dtype=jnp.int32), jnp.arange(1, half_steps, dtype=jnp.int32)]
    )
    angle = (frequency[:, None] * steps_line[None, :] % horizon).astype(jnp.float32) * (
        2.0 * math.pi / horizon
    )
    cosine_rows = (steps_line <= half_steps)[:, None]
    forward = jnp.where(cosine_rows, jnp.cos(angle), -jnp.sin(angle))
    edge_rows = (frequency == 0) | (frequency == half_steps)
    row_weight = (jnp.where(edge_rows, 1.0, 2.0).astype(jnp.float32) / horizon)[:, None]
    kernel_spectrum = jnp.dot(
        forward, smoother.T, precision=lax.Precision.HIGHEST, preferred_element_type=jnp.float32
    )
    class_table = (
        my_class[None, :] == jnp.arange(smoother.shape[0], dtype=jnp.int32)[:, None]
    ).astype(jnp.float32)
    unit_spectrum = jnp.dot(
        kernel_spectrum,
        class_table,
        precision=lax.Precision.HIGHEST,
        preferred_element_type=jnp.float32,
    )
    empty_row = jnp.zeros((1, unit_width), jnp.float32)
    kernel_real = unit_spectrum[: half_steps + 1]
    kernel_imag = jnp.concatenate([empty_row, unit_spectrum[half_steps + 1 :], empty_row], axis=0)
    row_table = (my_rows[:, None] == jnp.arange(row_blocks, dtype=jnp.int32)[None, :]).astype(jnp.float32)
    slot_table = (
        slot_of_tile[:, None] == jnp.arange(area_devices * capacity, dtype=jnp.int32)[None, :]
    ).astype(jnp.float32)
    block_table = (send_block[:, None] == jnp.arange(col_blocks, dtype=jnp.int32)[None, :]).astype(jnp.float32)
    lo_row = (unit_bus % panel_width).reshape(1, unit_area)
    hi_row = (unit_bus // panel_width).reshape(1, unit_area)
    lo_col = lo_row.reshape(unit_area, 1)
    power_time = jnp.zeros((block_steps, unit_area), jnp.float32)
    line_duals = jnp.zeros((block_steps, line_limit.shape[0]), jnp.float32)
    totals = []
    for repeat in range(ITERATIONS):
        if repeat == 0:
            injection = demand.astype(jnp.bfloat16)
        else:
            injection = (demand + units_to_bus(power_time, lo_col, hi_row, col_blocks, panel_width)).astype(
                jnp.bfloat16
            )
        sending = jnp.take(injection.reshape(block_steps, col_blocks, panel_width), send_block, axis=1)
        arrived = lax.all_to_all(
            sending.reshape(block_steps, area_devices, capacity, panel_width),
            AREA,
            split_axis=1,
            concat_axis=1,
            tiled=True,
        )
        panels = jnp.take(
            arrived.reshape(block_steps, area_devices * capacity, panel_width), slot_of_tile, axis=1
        )
        partial_value = jnp.einsum(
            "tjb,jlb->tjl", panels, ptdf_tiles, preferred_element_type=jnp.float32
        )
        line_flows = jnp.einsum(
            "tjl,jr->trl", partial_value, row_table, precision=lax.Precision.HIGHEST,
            preferred_element_type=jnp.float32,
        )
        line_flows = line_flows.reshape(block_steps, row_blocks * line_block)
        limits = line_limit[None, :]
        clipped = jnp.clip(line_flows + line_duals, -limits, limits)
        line_duals = line_duals + line_flows - clipped
        excess = line_flows - clipped
        local_total = jnp.sum(excess * excess)
        totals.append(local_total)
        weights = (line_duals + line_flows - clipped).astype(jnp.bfloat16)
        picked = jnp.take(weights.reshape(block_steps, row_blocks, line_block), my_rows, axis=1)
        contrib = jnp.einsum("tjl,jlb->tjb", picked, ptdf_tiles, preferred_element_type=jnp.float32)
        outbound = jnp.einsum(
            "tjb,js->tsb", contrib, slot_table, precision=lax.Precision.HIGHEST,
            preferred_element_type=jnp.float32,
        )
        outbound = outbound.reshape(block_steps, area_devices, capacity, panel_width)
        last = repeat == ITERATIONS - 1
        if last:
            extra = (
                jnp.zeros((block_steps, area_devices, 1, panel_width), jnp.float32)
                .at[0, :, 0, :ITERATIONS]
                .set(jnp.broadcast_to(jnp.stack(totals), (area_devices, ITERATIONS)))
            )
            outbound = jnp.concatenate([outbound, extra], axis=2)
        returned = lax.all_to_all(outbound, AREA, split_axis=1, concat_axis=1, tiled=True)
        if last:
            area_totals = jnp.sum(returned[0, :, capacity, :ITERATIONS], axis=0)
            returned = returned[:, :, :capacity]
        prices = jnp.einsum(
            "tsb,sc->tcb",
            returned.reshape(block_steps, area_devices * capacity, panel_width),
            block_table,
            precision=lax.Precision.HIGHEST,
            preferred_element_type=jnp.float32,
        )
        prices = prices.reshape(block_steps, bus_area)
        gradient = unit_cost + rho_weight * bus_to_units(prices, lo_row, hi_row)
        target = power_time - step_size * gradient
        columns = lax.all_to_all(target, TM, split_axis=1, concat_axis=0, tiled=True)
        spectrum = jnp.dot(
            forward, columns, precision=lax.Precision.HIGHEST, preferred_element_type=jnp.float32
        )
        spectrum_real = spectrum[: half_steps + 1]
        spectrum_imag = jnp.concatenate([empty_row, spectrum[half_steps + 1 :], empty_row], axis=0)
        product_real = spectrum_real * kernel_real - spectrum_imag * kernel_imag
        product_imag = spectrum_real * kernel_imag + spectrum_imag * kernel_real
        stacked = jnp.concatenate([product_real, product_imag[1:half_steps]], axis=0) * row_weight
        smoothed = lax.dot_general(
            forward,
            stacked,
            (((0,), (0,)), ((), ())),
            precision=lax.Precision.HIGHEST,
            preferred_element_type=jnp.float32,
        )
        power_cols = jnp.clip(smoothed, -my_cap[None, :], my_cap[None, :])
        if last:
            chunks = power_cols.reshape(time_devices, block_steps, unit_width)
            extra = (
                jnp.zeros((time_devices, 1, unit_width), jnp.float32)
                .at[:, 0, :ITERATIONS]
                .set(jnp.broadcast_to(area_totals, (time_devices, ITERATIONS)))
            )
            received = lax.all_to_all(
                jnp.concatenate([chunks, extra], axis=1), TM, split_axis=0, concat_axis=0, tiled=True
            )
            summed = jnp.sum(received[:, block_steps, :ITERATIONS], axis=0)
            power_time = jnp.transpose(received[:, :block_steps], (1, 0, 2)).reshape(block_steps, unit_area)
        else:
            power_time = lax.all_to_all(power_cols, TM, split_axis=0, concat_axis=1, tiled=True)
    entries = float(horizon * line_limit.shape[0] * area_devices)
    primal_rms = jnp.sqrt(summed / entries)
    return (power_time, line_duals, primal_rms)


def solution(mesh):
    finer = Mesh(mesh.devices.reshape(16, 4, 4, 2), ("tm_0", "tm_1", "area_0", "area_1"))
    placed = (
        P(TM, AREA),
        P(TM, AREA),
        P(AREA, None, None),
        P(),
        P(),
        P(),
        P(AREA),
        P(AREA),
        P(AREA),
        P(AREA),
        P(),
    )
    return jax.shard_map(
        per_device,
        mesh=finer,
        in_specs=placed,
        out_specs=(P(TM, AREA), P(TM, AREA), P()),
        check_vma=False,
    )
```

```python
import functools
import math

import jax
import jax.numpy as jnp
from jax import lax
from jax.sharding import Mesh
from jax.sharding import PartitionSpec as P
from jax.experimental import pallas as pl

ITERATIONS = 2
TM = ("tm_0", "tm_1")
AREA = ("area_0", "area_1")
TM_AREA = ("tm_0", "tm_1", "area_0", "area_1")


step_size = 0.5
rho_weight = 1.0


def laid_out(tiles, dim):
    dims = list(tiles.shape[1:])
    dims[dim] *= tiles.shape[0]
    return jnp.moveaxis(tiles, 0, dim).reshape(dims)


def copy_for_each(array, axis):
    count = lax.axis_size(axis)
    return lax.all_to_all(
        jnp.broadcast_to(array[None], (count, *array.shape)), axis, 0, 0, tiled=True
    )


def collect(array, axis, dim):
    return laid_out(copy_for_each(array, axis), dim)


PARTS = 2
ROWS = 16
UNIT_BLOCK = 8192


def split_parts(values):
    pieces = []
    rest = values
    for _ in range(PARTS):
        piece = rest.astype(jnp.bfloat16)
        pieces.append(piece)
        rest = rest - piece.astype(jnp.float32)
    return pieces


def group_targets(group):
    half = (lax.broadcasted_iota(jnp.int32, (ROWS, 1), 0) >= ROWS // 2).astype(jnp.int32)
    return 2 * group + half


def gather_kernel(table_ref, lo_ref, hi_ref, out_ref):
    lanes = table_ref.shape[1]
    width = lo_ref.shape[1]
    onehot = (lax.broadcasted_iota(jnp.int32, (lanes, width), 0) == lo_ref[...]).astype(jnp.bfloat16)
    picked = jnp.dot(table_ref[...], onehot, preferred_element_type=jnp.float32)
    hi = hi_ref[...]
    total = jnp.zeros((ROWS, width), jnp.float32)
    for group in range(table_ref.shape[0] // ROWS):
        block = picked[group * ROWS : (group + 1) * ROWS]
        total = total + jnp.where(hi == group_targets(group), block, 0.0)
    out_ref[...] = total


def bus_to_units(prices, lo_row, hi_row):
    steps, buses = prices.shape
    panel = 256
    blocks = buses // panel
    groups = (blocks + 1) // 2
    units = lo_row.shape[1]
    pieces = jnp.stack(split_parts(prices.reshape(steps, blocks, panel)), axis=0)
    pieces = jnp.pad(pieces, ((0, 0), (0, 0), (0, 2 * groups - blocks), (0, 0)))
    pieces = pieces.reshape(PARTS, steps, groups, 2, panel)
    table = jnp.transpose(pieces, (2, 3, 0, 1, 4)).reshape(groups * ROWS, panel)
    picked = pl.pallas_call(
        gather_kernel,
        grid=(units // UNIT_BLOCK,),
        in_specs=[
            pl.BlockSpec((groups * ROWS, panel), lambda i: (0, 0)),
            pl.BlockSpec((1, UNIT_BLOCK), lambda i: (0, i)),
            pl.BlockSpec((1, UNIT_BLOCK), lambda i: (0, i)),
        ],
        out_specs=pl.BlockSpec((ROWS, UNIT_BLOCK), lambda i: (0, i)),
        out_shape=jax.ShapeDtypeStruct((ROWS, units), jnp.float32),
    )(table, lo_row, hi_row)
    return jnp.sum(picked.reshape(ROWS // steps, steps, units), axis=0)


def scatter_kernel(parts_ref, lo_ref, hi_ref, out_ref):
    @pl.when(pl.program_id(0) == 0)
    def _():
        out_ref[...] = jnp.zeros(out_ref.shape, out_ref.dtype)

    width = parts_ref.shape[1]
    lanes = out_ref.shape[1]
    onehot = (lax.broadcasted_iota(jnp.int32, (width, lanes), 1) == lo_ref[...]).astype(jnp.bfloat16)
    parts = parts_ref[...]
    hi = hi_ref[...]
    masked = jnp.concatenate(
        [
            jnp.where(hi == group_targets(group), parts, jnp.zeros_like(parts))
            for group in range(out_ref.shape[0] // ROWS)
        ],
        axis=0,
    )
    out_ref[...] += jnp.dot(masked, onehot, preferred_element_type=jnp.float32)


def units_to_bus(power, lo_col, hi_row, blocks, panel):
    steps, units = power.shape
    groups = (blocks + 1) // 2
    pieces = split_parts(power)
    parts = jnp.concatenate(pieces + pieces, axis=0)
    summed = pl.pallas_call(
        scatter_kernel,
        grid=(units // UNIT_BLOCK,),
        in_specs=[
            pl.BlockSpec((ROWS, UNIT_BLOCK), lambda i: (0, i)),
            pl.BlockSpec((UNIT_BLOCK, 1), lambda i: (i, 0)),
            pl.BlockSpec((1, UNIT_BLOCK), lambda i: (0, i)),
        ],
        out_specs=pl.BlockSpec((groups * ROWS, panel), lambda i: (0, 0)),
        out_shape=jax.ShapeDtypeStruct((groups * ROWS, panel), jnp.float32),
    )(parts, lo_col, hi_row)
    summed = jnp.sum(summed.reshape(groups, 2, PARTS, steps, panel), axis=2)
    summed = jnp.transpose(summed, (2, 0, 1, 3)).reshape(steps, 2 * groups * panel)
    return summed[:, : blocks * panel]


def one_axis_at_a_time(array, axes):
    return functools.reduce(lax.psum, axes, array)


def per_device(
    demand,
    unit_cost,
    ptdf_tiles,
    tile_area,
    tile_block,
    tile_row,
    unit_bus,
    unit_class,
    power_cap,
    line_limit,
    smoother,
):
    time_devices = lax.axis_size(TM)
    area_devices = lax.axis_size(AREA)
    block_steps, bus_area = demand.shape
    unit_area = unit_cost.shape[1]
    tile_count, line_block, panel_width = ptdf_tiles.shape
    col_blocks = bus_area // panel_width
    row_blocks = line_limit.shape[0] // line_block
    capacity = 2 * tile_count // area_devices
    horizon = block_steps * time_devices
    unit_width = unit_area // time_devices
    area_index = lax.axis_index(AREA)
    time_index = lax.axis_index(TM)
    tile_areas = tile_area.reshape(area_devices, tile_count)
    block_grid = tile_block.reshape(area_devices, tile_count)
    row_grid = tile_row.reshape(area_devices, tile_count)
    is_source = (tile_areas == area_index).astype(jnp.int32)
    rank_source = jnp.cumsum(is_source, axis=1) - 1
    slot_ids = jnp.arange(capacity, dtype=jnp.int32)
    chosen = is_source[:, None, :] * (rank_source[:, None, :] == slot_ids[None, :, None]).astype(
        jnp.int32
    )
    send_block = jnp.sum(chosen * block_grid[:, None, :], axis=2).reshape(-1)
    my_areas = lax.dynamic_index_in_dim(tile_areas, area_index, 0, keepdims=False)
    my_blocks = lax.dynamic_index_in_dim(block_grid, area_index, 0, keepdims=False)
    my_rows = lax.dynamic_index_in_dim(row_grid, area_index, 0, keepdims=False)
    positions = jnp.arange(tile_count, dtype=jnp.int32)
    earlier = positions[None, :] <= positions[:, None]
    same_area = my_areas[None, :] == my_areas[:, None]
    rank_mine = jnp.sum((same_area & earlier).astype(jnp.int32), axis=1) - 1
    slot_of_tile = my_areas * capacity + rank_mine
    my_columns = my_areas * col_blocks + my_blocks
    my_class = lax.dynamic_slice_in_dim(unit_class, time_index * unit_width, unit_width)
    my_cap = lax.dynamic_slice_in_dim(power_cap, time_index * unit_width, unit_width)
    half_steps = horizon // 2
    steps_line = jnp.arange(horizon, dtype=jnp.int32)
    frequency = jnp.concatenate(
        [jnp.arange(half_steps + 1, dtype=jnp.int32), jnp.arange(1, half_steps, dtype=jnp.int32)]
    )
    angle = (frequency[:, None] * steps_line[None, :] % horizon).astype(jnp.float32) * (
        2.0 * math.pi / horizon
    )
    cosine_rows = (steps_line <= half_steps)[:, None]
    forward = jnp.where(cosine_rows, jnp.cos(angle), -jnp.sin(angle))
    edge_rows = (frequency == 0) | (frequency == half_steps)
    row_weight = (jnp.where(edge_rows, 1.0, 2.0).astype(jnp.float32) / horizon)[:, None]
    kernel_spectrum = jnp.dot(
        forward, smoother.T, precision=lax.Precision.HIGHEST, preferred_element_type=jnp.float32
    )
    class_table = (
        my_class[None, :] == jnp.arange(smoother.shape[0], dtype=jnp.int32)[:, None]
    ).astype(jnp.float32)
    unit_spectrum = jnp.dot(
        kernel_spectrum,
        class_table,
        precision=lax.Precision.HIGHEST,
        preferred_element_type=jnp.float32,
    )
    empty_row = jnp.zeros((1, unit_width), jnp.float32)
    kernel_real = unit_spectrum[: half_steps + 1]
    kernel_imag = jnp.concatenate([empty_row, unit_spectrum[half_steps + 1 :], empty_row], axis=0)
    row_table = (my_rows[:, None] == jnp.arange(row_blocks, dtype=jnp.int32)[None, :]).astype(jnp.float32)
    slot_table = (
        slot_of_tile[:, None] == jnp.arange(area_devices * capacity, dtype=jnp.int32)[None, :]
    ).astype(jnp.float32)
    block_table = (send_block[:, None] == jnp.arange(col_blocks, dtype=jnp.int32)[None, :]).astype(jnp.float32)
    lo_row = (unit_bus % panel_width).reshape(1, unit_area)
    hi_row = (unit_bus // panel_width).reshape(1, unit_area)
    lo_col = lo_row.reshape(unit_area, 1)
    power_time = jnp.zeros((block_steps, unit_area), jnp.float32)
    line_duals = jnp.zeros((block_steps, line_limit.shape[0]), jnp.float32)
    totals = []
    for repeat in range(ITERATIONS):
        if repeat == 0:
            injection = demand.astype(jnp.bfloat16)
        else:
            injection = (demand + units_to_bus(power_time, lo_col, hi_row, col_blocks, panel_width)).astype(
                jnp.bfloat16
            )
        sending = jnp.take(injection.reshape(block_steps, col_blocks, panel_width), send_block, axis=1)
        arrived = lax.all_to_all(
            sending.reshape(block_steps, area_devices, capacity, panel_width),
            AREA,
            split_axis=1,
            concat_axis=1,
            tiled=True,
        )
        panels = jnp.take(
            arrived.reshape(block_steps, area_devices * capacity, panel_width), slot_of_tile, axis=1
        )
        partial_value = jnp.einsum(
            "tjb,jlb->tjl", panels, ptdf_tiles, preferred_element_type=jnp.float32
        )
        line_flows = jnp.einsum(
            "tjl,jr->trl", partial_value, row_table, precision=lax.Precision.HIGHEST,
            preferred_element_type=jnp.float32,
        )
        line_flows = line_flows.reshape(block_steps, row_blocks * line_block)
        limits = line_limit[None, :]
        clipped = jnp.clip(line_flows + line_duals, -limits, limits)
        line_duals = line_duals + line_flows - clipped
        excess = line_flows - clipped
        local_total = jnp.sum(excess * excess)
        totals.append(local_total)
        weights = (line_duals + line_flows - clipped).astype(jnp.bfloat16)
        picked = jnp.take(weights.reshape(block_steps, row_blocks, line_block), my_rows, axis=1)
        contrib = jnp.einsum("tjl,jlb->tjb", picked, ptdf_tiles, preferred_element_type=jnp.float32)
        outbound = jnp.einsum(
            "tjb,js->tsb", contrib, slot_table, precision=lax.Precision.HIGHEST,
            preferred_element_type=jnp.float32,
        )
        outbound = outbound.reshape(block_steps, area_devices, capacity, panel_width)
        last = repeat == ITERATIONS - 1
        if last:
            extra = (
                jnp.zeros((block_steps, area_devices, 1, panel_width), jnp.float32)
                .at[0, :, 0, :ITERATIONS]
                .set(jnp.broadcast_to(jnp.stack(totals), (area_devices, ITERATIONS)))
            )
            outbound = jnp.concatenate([outbound, extra], axis=2)
        returned = lax.all_to_all(outbound, AREA, split_axis=1, concat_axis=1, tiled=True)
        if last:
            area_totals = jnp.sum(returned[0, :, capacity, :ITERATIONS], axis=0)
            returned = returned[:, :, :capacity]
        prices = jnp.einsum(
            "tsb,sc->tcb",
            returned.reshape(block_steps, area_devices * capacity, panel_width),
            block_table,
            precision=lax.Precision.HIGHEST,
            preferred_element_type=jnp.float32,
        )
        prices = prices.reshape(block_steps, bus_area)
        gradient = unit_cost + rho_weight * bus_to_units(prices, lo_row, hi_row)
        target = power_time - step_size * gradient
        columns = lax.all_to_all(target, TM, split_axis=1, concat_axis=0, tiled=True)
        spectrum = jnp.dot(
            forward, columns, precision=lax.Precision.HIGHEST, preferred_element_type=jnp.float32
        )
        spectrum_real = spectrum[: half_steps + 1]
        spectrum_imag = jnp.concatenate([empty_row, spectrum[half_steps + 1 :], empty_row], axis=0)
        product_real = spectrum_real * kernel_real - spectrum_imag * kernel_imag
        product_imag = spectrum_real * kernel_imag + spectrum_imag * kernel_real
        stacked = jnp.concatenate([product_real, product_imag[1:half_steps]], axis=0) * row_weight
        smoothed = lax.dot_general(
            forward,
            stacked,
            (((0,), (0,)), ((), ())),
            precision=lax.Precision.HIGHEST,
            preferred_element_type=jnp.float32,
        )
        power_cols = jnp.clip(smoothed, -my_cap[None, :], my_cap[None, :])
        if last:
            chunks = power_cols.reshape(time_devices, block_steps, unit_width)
            extra = (
                jnp.zeros((time_devices, 1, unit_width), jnp.float32)
                .at[:, 0, :ITERATIONS]
                .set(jnp.broadcast_to(area_totals, (time_devices, ITERATIONS)))
            )
            received = lax.all_to_all(
                jnp.concatenate([chunks, extra], axis=1), TM, split_axis=0, concat_axis=0, tiled=True
            )
            summed = jnp.sum(received[:, block_steps, :ITERATIONS], axis=0)
            power_time = jnp.transpose(received[:, :block_steps], (1, 0, 2)).reshape(block_steps, unit_area)
        else:
            power_time = lax.all_to_all(power_cols, TM, split_axis=0, concat_axis=1, tiled=True)
    entries = float(horizon * line_limit.shape[0] * area_devices)
    primal_rms = jnp.sqrt(summed / entries)
    return (power_time, line_duals, primal_rms)


def solution(mesh):
    finer = Mesh(mesh.devices.reshape(16, 4, 4, 2), ("tm_0", "tm_1", "area_0", "area_1"))
    placed = (
        P(TM, AREA),
        P(TM, AREA),
        P(AREA, None, None),
        P(),
        P(),
        P(),
        P(AREA),
        P(AREA),
        P(AREA),
        P(AREA),
        P(),
    )
    return jax.shard_map(
        per_device,
        mesh=finer,
        in_specs=placed,
        out_specs=(P(TM, AREA), P(TM, AREA), P()),
        check_vma=False,
    )
```

```python
import functools
import math

import jax
import jax.numpy as jnp
from jax import lax
from jax.sharding import Mesh
from jax.sharding import PartitionSpec as P
from jax.experimental import pallas as pl

ITERATIONS = 2
TM = ("tm_0", "tm_1")
AREA = ("area_0", "area_1")
TM_AREA = ("tm_0", "tm_1", "area_0", "area_1")


step_size = 0.5
rho_weight = 1.0


def laid_out(tiles, dim):
    dims = list(tiles.shape[1:])
    dims[dim] *= tiles.shape[0]
    return jnp.moveaxis(tiles, 0, dim).reshape(dims)


def copy_for_each(array, axis):
    count = lax.axis_size(axis)
    return lax.all_to_all(
        jnp.broadcast_to(array[None], (count, *array.shape)), axis, 0, 0, tiled=True
    )


def collect(array, axis, dim):
    return laid_out(copy_for_each(array, axis), dim)


PARTS = 2
ROWS = 16
UNIT_BLOCK = 4096


def split_parts(values):
    pieces = []
    rest = values
    for _ in range(PARTS):
        piece = rest.astype(jnp.bfloat16)
        pieces.append(piece)
        rest = rest - piece.astype(jnp.float32)
    return pieces


def group_targets(group):
    half = (lax.broadcasted_iota(jnp.int32, (ROWS, 1), 0) >= ROWS // 2).astype(jnp.int32)
    return 2 * group + half


def gather_kernel(table_ref, lo_ref, hi_ref, power_ref, cost_ref, out_ref):
    lanes = table_ref.shape[1]
    width = lo_ref.shape[1]
    onehot = (lax.broadcasted_iota(jnp.int32, (lanes, width), 0) == lo_ref[...]).astype(jnp.bfloat16)
    picked = jnp.dot(table_ref[...], onehot, preferred_element_type=jnp.float32)
    hi = hi_ref[...]
    total = jnp.zeros((ROWS, width), jnp.float32)
    for group in range(table_ref.shape[0] // ROWS):
        block = picked[group * ROWS : (group + 1) * ROWS]
        total = total + jnp.where(hi == group_targets(group), block, 0.0)
    quarter = ROWS // 4
    price = total[0:quarter] + total[quarter : 2 * quarter] + total[2 * quarter : 3 * quarter] + total[3 * quarter :]
    out_ref[...] = power_ref[...] - step_size * (cost_ref[...] + rho_weight * price)


def bus_to_units(prices, lo_row, hi_row, power, cost):
    steps, buses = prices.shape
    panel = 256
    blocks = buses // panel
    groups = (blocks + 1) // 2
    units = lo_row.shape[1]
    pieces = jnp.stack(split_parts(prices.reshape(steps, blocks, panel)), axis=0)
    pieces = jnp.pad(pieces, ((0, 0), (0, 0), (0, 2 * groups - blocks), (0, 0)))
    pieces = pieces.reshape(PARTS, steps, groups, 2, panel)
    table = jnp.transpose(pieces, (2, 3, 0, 1, 4)).reshape(groups * ROWS, panel)
    picked = pl.pallas_call(
        gather_kernel,
        grid=(units // UNIT_BLOCK,),
        in_specs=[
            pl.BlockSpec((groups * ROWS, panel), lambda i: (0, 0)),
            pl.BlockSpec((1, UNIT_BLOCK), lambda i: (0, i)),
            pl.BlockSpec((1, UNIT_BLOCK), lambda i: (0, i)),
            pl.BlockSpec((steps, UNIT_BLOCK), lambda i: (0, i)),
            pl.BlockSpec((steps, UNIT_BLOCK), lambda i: (0, i)),
        ],
        out_specs=pl.BlockSpec((steps, UNIT_BLOCK), lambda i: (0, i)),
        out_shape=jax.ShapeDtypeStruct((steps, units), jnp.float32),
    )(table, lo_row, hi_row, power, cost)
    return picked


def scatter_kernel(parts_ref, lo_ref, hi_ref, out_ref):
    @pl.when(pl.program_id(0) == 0)
    def _():
        out_ref[...] = jnp.zeros(out_ref.shape, out_ref.dtype)

    width = parts_ref.shape[1]
    lanes = out_ref.shape[1]
    onehot = (lax.broadcasted_iota(jnp.int32, (width, lanes), 1) == lo_ref[...]).astype(jnp.bfloat16)
    parts = parts_ref[...]
    hi = hi_ref[...]
    masked = jnp.concatenate(
        [
            jnp.where(hi == group_targets(group), parts, jnp.zeros_like(parts))
            for group in range(out_ref.shape[0] // ROWS)
        ],
        axis=0,
    )
    out_ref[...] += jnp.dot(masked, onehot, preferred_element_type=jnp.float32)


def units_to_bus(power, lo_col, hi_row, blocks, panel):
    steps, units = power.shape
    groups = (blocks + 1) // 2
    pieces = split_parts(power)
    parts = jnp.concatenate(pieces + pieces, axis=0)
    summed = pl.pallas_call(
        scatter_kernel,
        grid=(units // UNIT_BLOCK,),
        in_specs=[
            pl.BlockSpec((ROWS, UNIT_BLOCK), lambda i: (0, i)),
            pl.BlockSpec((UNIT_BLOCK, 1), lambda i: (i, 0)),
            pl.BlockSpec((1, UNIT_BLOCK), lambda i: (0, i)),
        ],
        out_specs=pl.BlockSpec((groups * ROWS, panel), lambda i: (0, 0)),
        out_shape=jax.ShapeDtypeStruct((groups * ROWS, panel), jnp.float32),
    )(parts, lo_col, hi_row)
    summed = jnp.sum(summed.reshape(groups, 2, PARTS, steps, panel), axis=2)
    summed = jnp.transpose(summed, (2, 0, 1, 3)).reshape(steps, 2 * groups * panel)
    return summed[:, : blocks * panel]


def one_axis_at_a_time(array, axes):
    return functools.reduce(lax.psum, axes, array)


def per_device(
    demand,
    unit_cost,
    ptdf_tiles,
    tile_area,
    tile_block,
    tile_row,
    unit_bus,
    unit_class,
    power_cap,
    line_limit,
    smoother,
):
    time_devices = lax.axis_size(TM)
    area_devices = lax.axis_size(AREA)
    block_steps, bus_area = demand.shape
    unit_area = unit_cost.shape[1]
    tile_count, line_block, panel_width = ptdf_tiles.shape
    col_blocks = bus_area // panel_width
    row_blocks = line_limit.shape[0] // line_block
    capacity = 2 * tile_count // area_devices
    horizon = block_steps * time_devices
    unit_width = unit_area // time_devices
    area_index = lax.axis_index(AREA)
    time_index = lax.axis_index(TM)
    tile_areas = tile_area.reshape(area_devices, tile_count)
    block_grid = tile_block.reshape(area_devices, tile_count)
    row_grid = tile_row.reshape(area_devices, tile_count)
    is_source = (tile_areas == area_index).astype(jnp.int32)
    rank_source = jnp.cumsum(is_source, axis=1) - 1
    slot_ids = jnp.arange(capacity, dtype=jnp.int32)
    chosen = is_source[:, None, :] * (rank_source[:, None, :] == slot_ids[None, :, None]).astype(
        jnp.int32
    )
    send_block = jnp.sum(chosen * block_grid[:, None, :], axis=2).reshape(-1)
    my_areas = lax.dynamic_index_in_dim(tile_areas, area_index, 0, keepdims=False)
    my_blocks = lax.dynamic_index_in_dim(block_grid, area_index, 0, keepdims=False)
    my_rows = lax.dynamic_index_in_dim(row_grid, area_index, 0, keepdims=False)
    positions = jnp.arange(tile_count, dtype=jnp.int32)
    earlier = positions[None, :] <= positions[:, None]
    same_area = my_areas[None, :] == my_areas[:, None]
    rank_mine = jnp.sum((same_area & earlier).astype(jnp.int32), axis=1) - 1
    slot_of_tile = my_areas * capacity + rank_mine
    my_columns = my_areas * col_blocks + my_blocks
    my_class = lax.dynamic_slice_in_dim(unit_class, time_index * unit_width, unit_width)
    my_cap = lax.dynamic_slice_in_dim(power_cap, time_index * unit_width, unit_width)
    half_steps = horizon // 2
    steps_line = jnp.arange(horizon, dtype=jnp.int32)
    frequency = jnp.concatenate(
        [jnp.arange(half_steps + 1, dtype=jnp.int32), jnp.arange(1, half_steps, dtype=jnp.int32)]
    )
    angle = (frequency[:, None] * steps_line[None, :] % horizon).astype(jnp.float32) * (
        2.0 * math.pi / horizon
    )
    cosine_rows = (steps_line <= half_steps)[:, None]
    forward = jnp.where(cosine_rows, jnp.cos(angle), -jnp.sin(angle))
    edge_rows = (frequency == 0) | (frequency == half_steps)
    row_weight = (jnp.where(edge_rows, 1.0, 2.0).astype(jnp.float32) / horizon)[:, None]
    kernel_spectrum = jnp.dot(
        forward, smoother.T, precision=lax.Precision.HIGHEST, preferred_element_type=jnp.float32
    )
    class_table = (
        my_class[None, :] == jnp.arange(smoother.shape[0], dtype=jnp.int32)[:, None]
    ).astype(jnp.float32)
    unit_spectrum = jnp.dot(
        kernel_spectrum,
        class_table,
        precision=lax.Precision.HIGHEST,
        preferred_element_type=jnp.float32,
    )
    empty_row = jnp.zeros((1, unit_width), jnp.float32)
    kernel_real = unit_spectrum[: half_steps + 1]
    kernel_imag = jnp.concatenate([empty_row, unit_spectrum[half_steps + 1 :], empty_row], axis=0)
    row_table = (my_rows[:, None] == jnp.arange(row_blocks, dtype=jnp.int32)[None, :]).astype(jnp.float32)
    slot_table = (
        slot_of_tile[:, None] == jnp.arange(area_devices * capacity, dtype=jnp.int32)[None, :]
    ).astype(jnp.float32)
    block_table = (send_block[:, None] == jnp.arange(col_blocks, dtype=jnp.int32)[None, :]).astype(jnp.float32)
    lo_row = (unit_bus % panel_width).reshape(1, unit_area)
    hi_row = (unit_bus // panel_width).reshape(1, unit_area)
    lo_col = lo_row.reshape(unit_area, 1)
    power_time = jnp.zeros((block_steps, unit_area), jnp.float32)
    line_duals = jnp.zeros((block_steps, line_limit.shape[0]), jnp.float32)
    totals = []
    for repeat in range(ITERATIONS):
        if repeat == 0:
            injection = demand.astype(jnp.bfloat16)
        else:
            injection = (demand + units_to_bus(power_time, lo_col, hi_row, col_blocks, panel_width)).astype(
                jnp.bfloat16
            )
        sending = jnp.take(injection.reshape(block_steps, col_blocks, panel_width), send_block, axis=1)
        arrived = lax.all_to_all(
            sending.reshape(block_steps, area_devices, capacity, panel_width),
            AREA,
            split_axis=1,
            concat_axis=1,
            tiled=True,
        )
        panels = jnp.take(
            arrived.reshape(block_steps, area_devices * capacity, panel_width), slot_of_tile, axis=1
        )
        partial_value = jnp.einsum(
            "tjb,jlb->tjl", panels, ptdf_tiles, preferred_element_type=jnp.float32
        )
        line_flows = jnp.einsum(
            "tjl,jr->trl", partial_value, row_table, precision=lax.Precision.HIGHEST,
            preferred_element_type=jnp.float32,
        )
        line_flows = line_flows.reshape(block_steps, row_blocks * line_block)
        limits = line_limit[None, :]
        clipped = jnp.clip(line_flows + line_duals, -limits, limits)
        line_duals = line_duals + line_flows - clipped
        excess = line_flows - clipped
        local_total = jnp.sum(excess * excess)
        totals.append(local_total)
        weights = (line_duals + line_flows - clipped).astype(jnp.bfloat16)
        picked = jnp.take(weights.reshape(block_steps, row_blocks, line_block), my_rows, axis=1)
        contrib = jnp.einsum("tjl,jlb->tjb", picked, ptdf_tiles, preferred_element_type=jnp.float32)
        outbound = jnp.einsum(
            "tjb,js->tsb", contrib, slot_table, precision=lax.Precision.HIGHEST,
            preferred_element_type=jnp.float32,
        )
        outbound = outbound.reshape(block_steps, area_devices, capacity, panel_width)
        last = repeat == ITERATIONS - 1
        if last:
            extra = (
                jnp.zeros((block_steps, area_devices, 1, panel_width), jnp.float32)
                .at[0, :, 0, :ITERATIONS]
                .set(jnp.broadcast_to(jnp.stack(totals), (area_devices, ITERATIONS)))
            )
            outbound = jnp.concatenate([outbound, extra], axis=2)
        returned = lax.all_to_all(outbound, AREA, split_axis=1, concat_axis=1, tiled=True)
        if last:
            area_totals = jnp.sum(returned[0, :, capacity, :ITERATIONS], axis=0)
            returned = returned[:, :, :capacity]
        prices = jnp.einsum(
            "tsb,sc->tcb",
            returned.reshape(block_steps, area_devices * capacity, panel_width),
            block_table,
            precision=lax.Precision.HIGHEST,
            preferred_element_type=jnp.float32,
        )
        prices = prices.reshape(block_steps, bus_area)
        target = bus_to_units(prices, lo_row, hi_row, power_time, unit_cost)
        columns = lax.all_to_all(target, TM, split_axis=1, concat_axis=0, tiled=True)
        spectrum = jnp.dot(
            forward, columns, precision=lax.Precision.HIGHEST, preferred_element_type=jnp.float32
        )
        spectrum_real = spectrum[: half_steps + 1]
        spectrum_imag = jnp.concatenate([empty_row, spectrum[half_steps + 1 :], empty_row], axis=0)
        product_real = spectrum_real * kernel_real - spectrum_imag * kernel_imag
        product_imag = spectrum_real * kernel_imag + spectrum_imag * kernel_real
        stacked = jnp.concatenate([product_real, product_imag[1:half_steps]], axis=0) * row_weight
        smoothed = lax.dot_general(
            forward,
            stacked,
            (((0,), (0,)), ((), ())),
            precision=lax.Precision.HIGHEST,
            preferred_element_type=jnp.float32,
        )
        power_cols = jnp.clip(smoothed, -my_cap[None, :], my_cap[None, :])
        if last:
            chunks = power_cols.reshape(time_devices, block_steps, unit_width)
            extra = (
                jnp.zeros((time_devices, 1, unit_width), jnp.float32)
                .at[:, 0, :ITERATIONS]
                .set(jnp.broadcast_to(area_totals, (time_devices, ITERATIONS)))
            )
            received = lax.all_to_all(
                jnp.concatenate([chunks, extra], axis=1), TM, split_axis=0, concat_axis=0, tiled=True
            )
            summed = jnp.sum(received[:, block_steps, :ITERATIONS], axis=0)
            power_time = jnp.transpose(received[:, :block_steps], (1, 0, 2)).reshape(block_steps, unit_area)
        else:
            power_time = lax.all_to_all(power_cols, TM, split_axis=0, concat_axis=1, tiled=True)
    entries = float(horizon * line_limit.shape[0] * area_devices)
    primal_rms = jnp.sqrt(summed / entries)
    return (power_time, line_duals, primal_rms)


def solution(mesh):
    finer = Mesh(mesh.devices.reshape(16, 4, 4, 2), ("tm_0", "tm_1", "area_0", "area_1"))
    placed = (
        P(TM, AREA),
        P(TM, AREA),
        P(AREA, None, None),
        P(),
        P(),
        P(),
        P(AREA),
        P(AREA),
        P(AREA),
        P(AREA),
        P(),
    )
    return jax.shard_map(
        per_device,
        mesh=finer,
        in_specs=placed,
        out_specs=(P(TM, AREA), P(TM, AREA), P()),
        check_vma=False,
    )
```
